512 devices in a mesh: seq: 128 (over z, y, core), head: 4 (over x).
Axes of the slice: x: 4, y: 8, z: 8, core: 2. Of those that a mesh axis runs over, the one named last changes fastest.
Arguments:
- hidden: bfloat16 [16384, 1024], P('seq', 'head'), may hold values from -6 to 6
- queries: bfloat16 [16384, 1024], P('seq', 'head'), may hold values from -40 to 40
- suffix_keys: bfloat16 [16384, 1024], P('seq', 'head'), may hold values from -4 to 4
- suffix_values: bfloat16 [16384, 1024], P('seq', 'head'), may hold values from -6 to 6
- lengths: int32 [128], P('seq'), may hold values from 1 to 128, 10240 in all
- key_cache: bfloat16 [128, 32, 1024], P('seq', None, 'head'), may hold values from -6 to 6
- value_cache: bfloat16 [128, 32, 1024], P('seq', None, 'head'), may hold values from -6 to 6
- page_group: int32 [128], replicated, may hold values from 0 to 3, as said below
- out_weight: bfloat16 [1024, 1024], P('head'), may hold values from -0.1875 to 0.1875
- norm_gain: float32 [1024], replicated, may hold values from 0.1 to 1.9
- router_weight: bfloat16 [1024, 16], P('head'), may hold values from -0.1875 to 0.1875
- routes: int32 [16384, 2], P('seq'), may hold values from 0 to 15, all different within a row; in each aligned block of 16 rows (0 to 15, 16 to 31, ...) at most 2 rows name the same one
- gate_weight: bfloat16 [128, 1024, 2816], P('seq', None, 'head'), as said below
- up_weight: bfloat16 [128, 1024, 2816], P('seq', None, 'head'), as said below
- down_weight: bfloat16 [128, 1024, 2816], P('seq', None, 'head'), as said below
- destinations: int32 [128], replicated, may hold values from 0 to 127, as said below
Outputs:
- layer_output: bfloat16 [16384, 1024], P('seq', 'head')
The draws below stay inside these ranges and needn't reach their ends.
Inputs may be any that keep to these rules, and one draw needn't show every extreme that they name: `lengths`: the largest length is 128. `page_group`: each of the 4 groups is named by exactly 32 entries. `routes`: each row names 2 different experts; in each aligned block of 16 rows no expert is named by more than 2 rows. `gate_weight`: copies h and h2 with h // 8 == h2 // 8 are equal. `up_weight`: copies h and h2 with h // 8 == h2 // 8 are equal. `down_weight`: copies h and h2 with h // 8 == h2 // 8 are equal. `destinations`: A permutation of the requests in which exactly 32 requests change place.
All inputs are finite; a program needn't handle non-finite values. No bound on the sum of `lengths` on one device may be relied on, other than what follows from the above.
Results may differ from the reference program's by a relative error of at most 0.0065.
Values may be sent and summed in bfloat16 or wider, within the bound.
No kernel may reach another device: no remote copies, remote signals or barrier semaphores. Data moves between devices by JAX's collectives and lax.ppermute only.
A program may use at most 64 MiB of HBM per device.

```python
import math
import jax
import jax.numpy as jnp
import numpy as np
from jax import lax

D = 1024
HEADS = 16
DH = 64
EXPERTS = 16
FF = 2816
TOPK = 2
ROWS = 128
PAGE = 32
GROUPS = 4
REQS = 128
TOKENS = 16384
PAGES = 128
GROUP_PAGES = 32
PREFIX = 1024
REPLICAS = 8
HOSTS = 128
SUB_ROWS = 16
CAP = 2
MIGRATE = 32


def attention_pair(key):
    key_queries, key_keys = jax.random.split(jax.random.fold_in(key, 11), 2)
    array_shape = (TOKENS, HEADS * DH)
    base_queries = jnp.clip(jax.random.normal(key_queries, array_shape, jnp.float32), -4.0, 4.0)
    base_keys = jnp.clip(jax.random.normal(key_keys, array_shape, jnp.float32), -4.0, 4.0)
    return (base_queries, base_keys)


def draw_queries(key, part):
    return attention_pair(key)[0].astype(jnp.bfloat16)


def draw_suffix_keys(key, part):
    return attention_pair(key)[1].astype(jnp.bfloat16)


def draw_page_group(key, part):
    shuffled = jax.random.permutation(jax.random.fold_in(key, 5), PAGES).astype(jnp.int32)
    return (shuffled // GROUP_PAGES).astype(jnp.int32)


def draw_destinations(key, part):
    shuffled = jax.random.permutation(jax.random.fold_in(key, 3), REQS).astype(jnp.int32)
    movers = shuffled[:MIGRATE]
    targets = jnp.roll(movers, 1)
    return jnp.arange(REQS, dtype=jnp.int32).at[movers].set(targets)


def placed_experts(key, salt, fan_in):
    base_key = jax.random.fold_in(key, salt)

    def one_copy(copy_index):
        expert_key = jax.random.fold_in(base_key, copy_index // REPLICAS)
        values = jax.random.normal(expert_key, (D, FF), jnp.float32)
        return jnp.clip(values, -6.0, 6.0) * fan_in ** (-0.5)
    return jax.lax.map(one_copy, jnp.arange(HOSTS, dtype=jnp.int32))


def draw_gate_weight(key, part):
    return placed_experts(key, 21, D).astype(jnp.bfloat16)


def draw_up_weight(key, part):
    return placed_experts(key, 22, D).astype(jnp.bfloat16)


def draw_down_weight(key, part):
    return placed_experts(key, 23, FF).astype(jnp.bfloat16)


def steps_of(rng, dims, pieces, smallest, high):
    level, own = 1.0, jax.random.fold_in(rng, 6)
    for dim, shards_of in pieces:
        heights = jnp.exp(jax.random.uniform(jax.random.fold_in(own, dim), (shards_of,), jnp.float32, smallest / len(pieces), high / len(pieces)))
        level = level * jnp.repeat(heights, dims[dim] // shards_of).reshape([-1 if axis == dim else 1 for axis in range(len(dims))])
    return level


def split_up(amount, total, reach, lean):
    weights = [(1 << 20) // math.isqrt(rank ** lean) + 1 for rank in range(2, amount + 1)]
    rest, given = total - reach - (amount - 1), [1] * (amount - 1)
    while rest > 0:
        free = [i for i in range(amount - 1) if given[i] < reach]
        whole, budget = sum([weights[i] for i in free]), rest
        for i in free:
            extra = min(reach - given[i], max(1, budget * weights[i] // whole), rest)
            given[i] = given[i] + extra
            rest = rest - extra
    return np.array([reach] + given)


def uneven(stream_key, count, total, reach, slope):
    if count == 2:
        one = jax.random.randint(stream_key, (), max(1, total - reach), min(reach, total - 1) + 1)
        return jnp.stack([one, total - one])
    sizes = jnp.asarray(split_up(count, total, reach, slope), jnp.int32)
    couples = (count - 1) // 2
    giver, taker = sizes[1:1 + 2 * couples:2], sizes[2:2 + 2 * couples:2]
    slack = jnp.minimum(giver - 1, reach - taker)
    shifted = jax.random.randint(jax.random.fold_in(stream_key, 1), (couples,), 0, 1 << 20) % (slack + 1)
    sizes = sizes.at[1:1 + 2 * couples:2].set(giver - shifted).at[2:2 + 2 * couples:2].set(taker + shifted)
    return sizes[jax.random.permutation(jax.random.fold_in(stream_key, 2), count)]


def shared_out(own_key, own, number, rows, amount, top, most, slope):
    sequence = jax.random.permutation(own_key, amount)
    crowded, ordinary = portions_of(amount, rows * top, most, slope, True), portions_of(amount, rows * top, most, slope, False)
    places = jnp.arange(amount)

    def named(sizes, rotation):
        used = int((sizes > 0).sum())
        fixed = max(1, used // 4)
        passed = fixed + (places - fixed + rotation * (used - fixed)) % max(1, amount - fixed)
        return jnp.zeros((amount,), jnp.int32).at[sequence[jnp.where(places < fixed, places, passed)]].set(jnp.asarray(sizes, jnp.int32))

    sizes = jnp.where(number % 4 == 0, named(crowded, number // 4), named(ordinary, number - number // 4 - 1))
    mixed = jax.random.permutation(jax.random.fold_in(own, 3), amount)
    giver, receiver = mixed[0:amount // 2 * 2:2], mixed[1:amount // 2 * 2:2]
    margin = jnp.minimum(sizes[giver] - 1, most - sizes[receiver]) // 2
    margin = jnp.where((giver == sequence[0]) | (receiver == sequence[0]) | (sizes[receiver] == 0), 0, jnp.maximum(margin, 0))
    passed = jax.random.randint(jax.random.fold_in(own, 4), (amount // 2,), 0, 1 << 20) % (margin + 1)
    sizes = sizes.at[giver].add(-passed).at[receiver].add(passed)
    labels = jnp.searchsorted(jnp.cumsum(sizes), jnp.arange(rows * top), side="right").astype(jnp.int32)
    grid = labels.reshape(top, rows).T
    grid = grid[jax.random.permutation(jax.random.fold_in(own, 1), rows)]
    rotation = jax.random.randint(jax.random.fold_in(own, 2), (rows, 1), 0, top)
    return jnp.take_along_axis(grid, (jnp.arange(top)[None, :] + rotation) % top, axis=1)


def portions_of(amount, total, reach, skew, full):
    portions = [(1 << 20) // math.isqrt(grade ** skew) + 1 for grade in range(1, amount + 1)]
    largest = reach if full else min(reach, max(-(-total // amount), total * portions[0] // sum(portions)))
    least = 1 if total - largest >= amount - 1 else 0
    given, spare = [largest] + [least] * (amount - 1), total - largest - least * (amount - 1)
    while spare > 0:
        movable = [i for i in range(1, amount) if given[i] < largest] or [i for i in range(1, amount) if given[i] < reach]
        whole, budget = sum([portions[i] for i in movable]), spare
        for i in movable:
            extra = min(reach - given[i], max(1, budget * portions[i] // whole), spare)
            given[i] = given[i] + extra
            spare = spare - extra
    return np.array(given)


def normal_values(rng, extent, scale, limit, shards=(), held_as=jnp.bfloat16):
    level = steps_of(rng, extent, shards, -0.22, 0.18) if shards else 1.0
    entries = jax.random.normal(rng, extent, jnp.float32) * scale * level
    return jnp.minimum(jnp.maximum(entries, -limit), limit).astype(held_as)


def setup_inputs(seed: int = 0) -> dict:
    streams_of = jax.random.split(jax.random.key(seed), 17)
    hidden = normal_values(streams_of[0], (TOKENS, D), 1.0, 6.0, ((0, 128), (1, 4)))
    queries = draw_queries(jax.random.fold_in(streams_of[16], 71), 0)
    suffix_keys = draw_suffix_keys(jax.random.fold_in(streams_of[16], 71), 0)
    suffix_values = normal_values(streams_of[3], (TOKENS, HEADS * DH), 1.0, 6.0, ((0, 128), (1, 4)))
    lengths = uneven(streams_of[4], REQS, REQS * ROWS * 5 // 8, ROWS, 1).astype(jnp.int32)
    key_cache = normal_values(streams_of[5], (PAGES, PAGE, HEADS * DH), 1.0, 6.0, ((0, 128), (2, 4)))
    value_cache = normal_values(streams_of[6], (PAGES, PAGE, HEADS * DH), 1.0, 6.0, ((0, 128), (2, 4)))
    page_group = draw_page_group(jax.random.fold_in(streams_of[16], 71), 0)
    out_weight = normal_values(streams_of[8], (HEADS * DH, D), (HEADS * DH) ** -0.5, 0.1875, ((0, 4),))
    norm_gain = jnp.clip(1.0 + 0.18 * jax.random.normal(streams_of[9], (D,), jnp.float32), 0.1, 1.9)
    router_weight = normal_values(streams_of[10], (D, EXPERTS), D ** -0.5, 0.1875, ((0, 4),))
    routes_keys = jax.random.split(jax.random.fold_in(streams_of[11], 1), TOKENS // SUB_ROWS)
    routes_turns = jax.random.permutation(jax.random.fold_in(streams_of[11], 3), TOKENS // SUB_ROWS)
    routes = jax.vmap(lambda own, number: shared_out(jax.random.fold_in(streams_of[11], 2), own, number, SUB_ROWS, EXPERTS, TOPK, CAP, 2))(routes_keys, routes_turns).reshape((TOKENS, TOPK))
    gate_weight = draw_gate_weight(jax.random.fold_in(streams_of[16], 71), 0)
    up_weight = draw_up_weight(jax.random.fold_in(streams_of[16], 71), 0)
    down_weight = draw_down_weight(jax.random.fold_in(streams_of[16], 71), 0)
    destinations = draw_destinations(jax.random.fold_in(streams_of[16], 71), 0)
    return {"hidden": hidden, "queries": queries, "suffix_keys": suffix_keys, "suffix_values": suffix_values, "lengths": lengths, "key_cache": key_cache, "value_cache": value_cache, "page_group": page_group, "out_weight": out_weight, "norm_gain": norm_gain, "router_weight": router_weight, "routes": routes, "gate_weight": gate_weight, "up_weight": up_weight, "down_weight": down_weight, "destinations": destinations}


norm_eps = 1e-06

def page_inverse(page_group, group_pages, groups):
    page_total = page_group.shape[0]
    onehot = (page_group[:, None] == jnp.arange(groups, dtype=jnp.int32)[None, :]).astype(jnp.int32)
    page_rank = lax.optimization_barrier(jnp.sum((jnp.cumsum(onehot, axis=0) - 1) * onehot, axis=1))
    target = page_group * group_pages + page_rank
    return jnp.zeros((page_total,), jnp.int32).at[target].set(jnp.arange(page_total, dtype=jnp.int32))

def attend_request(query_rows, key_rows, value_rows, prefix_keys, prefix_values, length, head_total):
    row_count = query_rows.shape[0]
    head_size = query_rows.shape[1] // head_total
    scale = head_size ** (-0.5)

    def heads_of(array):
        return array.reshape(array.shape[0], head_total, head_size).astype(jnp.float32)
    prefix_scores = jnp.einsum('qhd,khd->hqk', heads_of(query_rows), heads_of(prefix_keys)) * scale
    suffix_scores = jnp.einsum('qhd,khd->hqk', heads_of(query_rows), heads_of(key_rows)) * scale
    query_pos = jnp.arange(row_count, dtype=jnp.int32)[:, None]
    key_pos = jnp.arange(row_count, dtype=jnp.int32)[None, :]
    allowed = (key_pos <= query_pos) & (key_pos < length)
    suffix_scores = jnp.where(allowed[None], suffix_scores, -jnp.inf)
    row_max = jnp.maximum(lax.optimization_barrier(jnp.max(prefix_scores, axis=2)), lax.optimization_barrier(jnp.max(suffix_scores, axis=2)))[..., None]
    prefix_exp = jnp.exp(prefix_scores - row_max)
    suffix_exp = jnp.exp(suffix_scores - row_max)
    denominators = lax.optimization_barrier(jnp.sum(prefix_exp, axis=2, keepdims=True)) + lax.optimization_barrier(jnp.sum(suffix_exp, axis=2, keepdims=True))
    prefix_probs = (prefix_exp / denominators).astype(jnp.bfloat16)
    suffix_probs = (suffix_exp / denominators).astype(jnp.bfloat16)
    mixed_heads = jnp.einsum('hqk,khd->qhd', prefix_probs.astype(jnp.float32), heads_of(prefix_values))
    mixed_heads = mixed_heads + jnp.einsum('hqk,khd->qhd', suffix_probs.astype(jnp.float32), heads_of(value_rows))
    return mixed_heads.reshape(row_count, head_total * head_size).astype(jnp.bfloat16)

def reference(hidden, queries, suffix_keys, suffix_values, lengths, key_cache, value_cache, page_group, out_weight, norm_gain, router_weight, routes, gate_weight, up_weight, down_weight, destinations):
    inverse = page_inverse(page_group, GROUP_PAGES, GROUPS)
    block_requests = REQS // GROUPS
    features = HEADS * DH

    def one_request(request):
        start = (request * ROWS).astype(jnp.int32)
        query_rows = lax.dynamic_slice_in_dim(queries, start, ROWS, 0)
        key_rows = lax.dynamic_slice_in_dim(suffix_keys, start, ROWS, 0)
        value_rows = lax.dynamic_slice_in_dim(suffix_values, start, ROWS, 0)
        group_index = (request // block_requests).astype(jnp.int32)
        page_index = lax.dynamic_slice_in_dim(inverse, group_index * GROUP_PAGES, GROUP_PAGES, 0)
        prefix_keys = jnp.take(key_cache, page_index, axis=0).reshape(PREFIX, features)
        prefix_values = jnp.take(value_cache, page_index, axis=0).reshape(PREFIX, features)
        return attend_request(query_rows, key_rows, value_rows, prefix_keys, prefix_values, lengths[request], HEADS)
    attended = lax.map(one_request, jnp.arange(REQS, dtype=jnp.int32)).reshape(TOKENS, features)
    resid = hidden.astype(jnp.float32) + jnp.dot(attended, out_weight, preferred_element_type=jnp.float32)
    normed = (resid * lax.rsqrt(lax.optimization_barrier(jnp.mean(resid * resid, axis=1, keepdims=True)) + norm_eps) * norm_gain).astype(jnp.bfloat16)
    logits = jnp.dot(normed, router_weight, preferred_element_type=jnp.float32)
    chosen = jnp.take_along_axis(logits, routes, axis=1)
    gate_first = jax.nn.sigmoid(chosen[:, 0] - chosen[:, 1])
    gate_second = jax.nn.sigmoid(chosen[:, 1] - chosen[:, 0])
    pair_total = TOKENS * TOPK
    expert_ids = routes.reshape(-1)
    order = jnp.argsort(expert_ids, stable=True).astype(jnp.int32)
    counts = lax.optimization_barrier(jnp.sum((expert_ids[:, None] == jnp.arange(EXPERTS, dtype=jnp.int32)[None, :]).astype(jnp.int32), axis=0))
    starts = (jnp.cumsum(counts) - counts).astype(jnp.int32)
    most_rows = REQS * REPLICAS * CAP
    padded_order = jnp.concatenate([order, jnp.zeros((most_rows,), jnp.int32)])

    def one_expert(expert):
        pair_index = lax.dynamic_slice_in_dim(padded_order, starts[expert], most_rows, 0)
        valid = jnp.arange(most_rows, dtype=jnp.int32) < counts[expert]
        token_rows = jnp.take(normed, pair_index // TOPK, axis=0)
        copy_index = expert * REPLICAS
        gate_act = jnp.dot(token_rows, gate_weight[copy_index], preferred_element_type=jnp.float32)
        up_act = jnp.dot(token_rows, up_weight[copy_index], preferred_element_type=jnp.float32)
        expert_hidden = (jax.nn.gelu(gate_act, approximate=True) * up_act).astype(jnp.bfloat16)
        expert_out = jnp.dot(expert_hidden, down_weight[copy_index].T, preferred_element_type=jnp.float32).astype(jnp.bfloat16)
        return (jnp.where(valid[:, None], expert_out, jnp.zeros_like(expert_out)), pair_index)
    outputs, pair_indices = lax.map(one_expert, jnp.arange(EXPERTS, dtype=jnp.int32))
    pair_out = jnp.zeros((pair_total, D), jnp.float32).at[pair_indices.reshape(-1)].add(outputs.reshape(-1, D).astype(jnp.float32))
    pair_out = pair_out.reshape(TOKENS, TOPK, D)
    layer = resid + gate_first[:, None] * pair_out[:, 0] + gate_second[:, None] * pair_out[:, 1]
    layer = layer.astype(jnp.bfloat16)
    positions = jnp.arange(ROWS, dtype=jnp.int32)
    live_rows = (positions[None, :] < lengths[:, None]).reshape(TOKENS)
    layer = jnp.where(live_rows[:, None], layer, jnp.zeros_like(layer))
    by_request = layer.reshape(REQS, ROWS, D)
    placed = jnp.zeros_like(by_request).at[destinations].set(by_request)
    return placed.reshape(TOKENS, D)
```

```python
import jax
import jax.numpy as jnp
from jax import lax
from jax.sharding import PartitionSpec as P

DH = 64
EXPERTS = 16
TOPK = 2
GROUPS = 4


norm_eps = 1e-06


def page_inverse(page_group, group_pages, groups):
    page_total = page_group.shape[0]
    onehot = (page_group[:, None] == jnp.arange(groups, dtype=jnp.int32)[None, :]).astype(jnp.int32)
    page_rank = jnp.sum((jnp.cumsum(onehot, axis=0) - 1) * onehot, axis=1)
    target = page_group * group_pages + page_rank
    return (
        jnp.zeros((page_total,), jnp.int32).at[target].set(jnp.arange(page_total, dtype=jnp.int32))
    )


def attend_rows(query_rows, key_rows, value_rows, prefix_keys, prefix_values, length, head_total):
    row_count = query_rows.shape[0]
    head_size = query_rows.shape[1] // head_total
    scale = head_size ** (-0.5)

    def heads_of(array):
        return array.reshape(array.shape[0], head_total, head_size)

    prefix_scores = (
        jnp.einsum(
            "qhd,khd->hqk",
            heads_of(query_rows),
            heads_of(prefix_keys),
            preferred_element_type=jnp.float32,
        )
        * scale
    )
    suffix_scores = (
        jnp.einsum(
            "qhd,khd->hqk",
            heads_of(query_rows),
            heads_of(key_rows),
            preferred_element_type=jnp.float32,
        )
        * scale
    )
    query_pos = jnp.arange(row_count, dtype=jnp.int32)[:, None]
    key_pos = jnp.arange(row_count, dtype=jnp.int32)[None, :]
    allowed = (key_pos <= query_pos) & (key_pos < length)
    suffix_scores = jnp.where(allowed[None], suffix_scores, -jnp.inf)
    row_max = jnp.maximum(jnp.max(prefix_scores, axis=2), jnp.max(suffix_scores, axis=2))[..., None]
    prefix_exp = jnp.exp(prefix_scores - row_max)
    suffix_exp = jnp.exp(suffix_scores - row_max)
    denominators = jnp.sum(prefix_exp, axis=2, keepdims=True) + jnp.sum(
        suffix_exp, axis=2, keepdims=True
    )
    prefix_probs = (prefix_exp / denominators).astype(jnp.bfloat16)
    suffix_probs = (suffix_exp / denominators).astype(jnp.bfloat16)
    mixed_heads = jnp.einsum(
        "hqk,khd->qhd", prefix_probs, heads_of(prefix_values), preferred_element_type=jnp.float32
    )
    mixed_heads = mixed_heads + jnp.einsum(
        "hqk,khd->qhd", suffix_probs, heads_of(value_rows), preferred_element_type=jnp.float32
    )
    return mixed_heads.reshape(row_count, head_total * head_size).astype(jnp.bfloat16)


def slot_table(route_rows, replicas, per_device, experts):
    row_count, topk_count = route_rows.shape
    sub_rows = row_count // replicas
    flat_routes = route_rows.reshape(replicas, sub_rows * topk_count)
    onehot = (flat_routes[..., None] == jnp.arange(experts, dtype=jnp.int32)).astype(jnp.int32)
    slot_rank = jnp.sum((jnp.cumsum(onehot, axis=1) - 1) * onehot, axis=2).reshape(-1)
    expert_flat = route_rows.reshape(-1)
    block_of = jnp.arange(row_count * topk_count, dtype=jnp.int32) // (sub_rows * topk_count)
    target_device = expert_flat // per_device * replicas + block_of
    local_slot = expert_flat % per_device
    return (target_device, local_slot, slot_rank)


def on_device(
    hidden,
    queries,
    suffix_keys,
    suffix_values,
    lengths,
    key_cache,
    value_cache,
    page_group,
    out_weight,
    norm_gain,
    router_weight,
    routes,
    gate_weight,
    up_weight,
    down_weight,
    destinations,
):
    seq_count = lax.axis_size("seq")
    head_count = lax.axis_size("head")
    seq_index = lax.axis_index("seq")
    head_index = lax.axis_index("head")
    row_count = hidden.shape[0]
    column_width = hidden.shape[1]
    features = queries.shape[1]
    local_heads = features // DH
    block_devices = seq_count // GROUPS
    page_local = key_cache.shape[0]
    page_rows = key_cache.shape[1]
    group_pages = page_local * block_devices
    replicas = max(1, seq_count // EXPERTS)
    per_device = max(1, EXPERTS // seq_count)
    capacity = 5 * row_count * TOPK // (4 * EXPERTS * replicas)
    inverse = page_inverse(page_group, group_pages, GROUPS)
    group_index = seq_index // block_devices
    half_width = page_rows * features
    local_pages = jnp.concatenate(
        [key_cache.reshape(page_local, half_width), value_cache.reshape(page_local, half_width)],
        axis=1,
    )
    all_pages = lax.all_gather(local_pages, "seq", axis=0, tiled=True)
    full_weight = lax.all_gather(out_weight, "head", axis=0, tiled=True)
    full_hidden = lax.all_gather(hidden, "head", axis=1, tiled=True)
    full_router = lax.all_gather(router_weight, "head", axis=0, tiled=True)
    chosen = lax.dynamic_slice_in_dim(inverse, group_index * group_pages, group_pages, 0)
    held_pages = jnp.take(all_pages, chosen, axis=0)
    prefix_keys = held_pages[:, :half_width].reshape(group_pages * page_rows, features)
    prefix_values = held_pages[:, half_width:].reshape(group_pages * page_rows, features)
    length = lengths[0]
    attended = attend_rows(
        queries, suffix_keys, suffix_values, prefix_keys, prefix_values, length, local_heads
    )
    full_attended = lax.all_gather(attended, "head", axis=1, tiled=True)
    resid = full_hidden.astype(jnp.float32) + jnp.dot(
        full_attended, full_weight, preferred_element_type=jnp.float32
    )
    normed = (
        resid * lax.rsqrt(jnp.mean(resid * resid, axis=1, keepdims=True) + norm_eps) * norm_gain
    ).astype(jnp.bfloat16)
    logits = jnp.dot(normed, full_router, preferred_element_type=jnp.float32)
    chosen_logits = jnp.take_along_axis(logits, routes, axis=1)
    gate_first = jax.nn.sigmoid(chosen_logits[:, 0] - chosen_logits[:, 1])
    gate_second = jax.nn.sigmoid(chosen_logits[:, 1] - chosen_logits[:, 0])
    target_device, local_slot, slot_rank = slot_table(routes, replicas, per_device, EXPERTS)
    slot_flat = (target_device * per_device + local_slot) * capacity + slot_rank
    slot_total = seq_count * per_device * capacity
    pair_count = row_count * TOPK
    slot_pair = (
        jnp.zeros((slot_total,), jnp.int32)
        .at[slot_flat]
        .set(jnp.arange(pair_count, dtype=jnp.int32), mode="drop")
    )
    send_rows = jnp.take(normed, slot_pair // TOPK, axis=0).reshape(
        seq_count, per_device, capacity, normed.shape[1]
    )
    slots = lax.all_to_all(send_rows, "seq", split_axis=0, concat_axis=0, tiled=True)
    gate_act = jnp.einsum("spnd,pdf->spnf", slots, gate_weight, preferred_element_type=jnp.float32)
    up_act = jnp.einsum("spnd,pdf->spnf", slots, up_weight, preferred_element_type=jnp.float32)
    expert_hidden = (jax.nn.gelu(gate_act, approximate=True) * up_act).astype(jnp.bfloat16)
    partial_out = jnp.einsum(
        "spnf,pdf->spnd", expert_hidden, down_weight, preferred_element_type=jnp.float32
    )
    part_dims = partial_out.shape
    split_part = partial_out.reshape(
        part_dims[0], part_dims[1], part_dims[2], head_count, part_dims[3] // head_count
    ).astype(jnp.bfloat16)
    by_head = lax.all_to_all(split_part, "head", split_axis=3, concat_axis=3, tiled=True)
    summed = jnp.sum(by_head.astype(jnp.float32), axis=3).astype(jnp.bfloat16)
    returned = lax.all_to_all(summed, "seq", split_axis=0, concat_axis=0, tiled=True)
    picked = (
        returned[target_device, local_slot, slot_rank]
        .astype(jnp.float32)
        .reshape(row_count, TOPK, column_width)
    )
    resid_columns = lax.dynamic_slice_in_dim(resid, head_index * column_width, column_width, 1)
    layer = resid_columns + gate_first[:, None] * picked[:, 0] + gate_second[:, None] * picked[:, 1]
    layer = layer.astype(jnp.bfloat16)
    live_rows = jnp.arange(row_count, dtype=jnp.int32) < length
    layer = jnp.where(live_rows[:, None], layer, jnp.zeros_like(layer))
    out_pieces = layer.reshape(seq_count, row_count // seq_count, column_width)
    scattered = lax.all_to_all(out_pieces, "seq", split_axis=0, concat_axis=0, tiled=True)
    inverse_destination = (
        jnp.zeros((seq_count,), jnp.int32)
        .at[destinations]
        .set(jnp.arange(seq_count, dtype=jnp.int32))
    )
    reordered = jnp.take(scattered, inverse_destination, axis=0)
    settled = lax.all_to_all(reordered, "seq", split_axis=0, concat_axis=0, tiled=True)
    return settled.reshape(row_count, column_width)


def solution(mesh):
    return jax.shard_map(
        on_device,
        mesh=mesh,
        in_specs=(
            P("seq", "head"),
            P("seq", "head"),
            P("seq", "head"),
            P("seq", "head"),
            P("seq"),
            P("seq", None, "head"),
            P("seq", None, "head"),
            P(),
            P("head", None),
            P(),
            P("head", None),
            P("seq", None),
            P("seq", None, "head"),
            P("seq", None, "head"),
            P("seq", None, "head"),
            P(),
        ),
        out_specs=P("seq", "head"),
        check_vma=False,
    )
```

```python
import jax
import jax.numpy as jnp
from jax import lax
from jax.sharding import PartitionSpec as P

DH = 64
EXPERTS = 16
TOPK = 2
GROUPS = 4


norm_eps = 1e-06


def page_inverse(page_group, group_pages, groups):
    page_total = page_group.shape[0]
    onehot = (page_group[:, None] == jnp.arange(groups, dtype=jnp.int32)[None, :]).astype(jnp.int32)
    page_rank = jnp.sum((jnp.cumsum(onehot, axis=0) - 1) * onehot, axis=1)
    target = page_group * group_pages + page_rank
    return (
        jnp.zeros((page_total,), jnp.int32).at[target].set(jnp.arange(page_total, dtype=jnp.int32))
    )


def attend_rows(query_rows, key_rows, value_rows, prefix_keys, prefix_values, length, head_total):
    row_count = query_rows.shape[0]
    head_size = query_rows.shape[1] // head_total
    scale = head_size ** (-0.5)

    def heads_of(array):
        return array.reshape(array.shape[0], head_total, head_size)

    prefix_scores = (
        jnp.einsum(
            "qhd,khd->hqk",
            heads_of(query_rows),
            heads_of(prefix_keys),
            preferred_element_type=jnp.float32,
        )
        * scale
    )
    suffix_scores = (
        jnp.einsum(
            "qhd,khd->hqk",
            heads_of(query_rows),
            heads_of(key_rows),
            preferred_element_type=jnp.float32,
        )
        * scale
    )
    query_pos = jnp.arange(row_count, dtype=jnp.int32)[:, None]
    key_pos = jnp.arange(row_count, dtype=jnp.int32)[None, :]
    allowed = (key_pos <= query_pos) & (key_pos < length)
    suffix_scores = jnp.where(allowed[None], suffix_scores, -jnp.inf)
    row_max = jnp.maximum(jnp.max(prefix_scores, axis=2), jnp.max(suffix_scores, axis=2))[..., None]
    prefix_exp = jnp.exp(prefix_scores - row_max)
    suffix_exp = jnp.exp(suffix_scores - row_max)
    denominators = jnp.sum(prefix_exp, axis=2, keepdims=True) + jnp.sum(
        suffix_exp, axis=2, keepdims=True
    )
    prefix_probs = (prefix_exp / denominators).astype(jnp.bfloat16)
    suffix_probs = (suffix_exp / denominators).astype(jnp.bfloat16)
    mixed_heads = jnp.einsum(
        "hqk,khd->qhd", prefix_probs, heads_of(prefix_values), preferred_element_type=jnp.float32
    )
    mixed_heads = mixed_heads + jnp.einsum(
        "hqk,khd->qhd", suffix_probs, heads_of(value_rows), preferred_element_type=jnp.float32
    )
    return mixed_heads.reshape(row_count, head_total * head_size).astype(jnp.bfloat16)


def slot_table(route_rows, replicas, per_device, experts):
    row_count, topk_count = route_rows.shape
    sub_rows = row_count // replicas
    flat_routes = route_rows.reshape(replicas, sub_rows * topk_count)
    onehot = (flat_routes[..., None] == jnp.arange(experts, dtype=jnp.int32)).astype(jnp.int32)
    slot_rank = jnp.sum((jnp.cumsum(onehot, axis=1) - 1) * onehot, axis=2).reshape(-1)
    expert_flat = route_rows.reshape(-1)
    block_of = jnp.arange(row_count * topk_count, dtype=jnp.int32) // (sub_rows * topk_count)
    target_device = expert_flat // per_device * replicas + block_of
    local_slot = expert_flat % per_device
    return (target_device, local_slot, slot_rank)


def on_device(
    hidden,
    queries,
    suffix_keys,
    suffix_values,
    lengths,
    key_cache,
    value_cache,
    page_group,
    out_weight,
    norm_gain,
    router_weight,
    routes,
    gate_weight,
    up_weight,
    down_weight,
    destinations,
):
    seq_count = lax.axis_size("seq")
    head_count = lax.axis_size("head")
    seq_index = lax.axis_index("seq")
    head_index = lax.axis_index("head")
    row_count = hidden.shape[0]
    column_width = hidden.shape[1]
    features = queries.shape[1]
    local_heads = features // DH
    block_devices = seq_count // GROUPS
    page_local = key_cache.shape[0]
    page_rows = key_cache.shape[1]
    group_pages = page_local * block_devices
    replicas = max(1, seq_count // EXPERTS)
    per_device = max(1, EXPERTS // seq_count)
    capacity = 5 * row_count * TOPK // (4 * EXPERTS * replicas)
    inverse = page_inverse(page_group, group_pages, GROUPS)
    inverse_destination = (
        jnp.zeros((seq_count,), jnp.int32)
        .at[destinations]
        .set(jnp.arange(seq_count, dtype=jnp.int32))
    )
    own_request = inverse_destination[seq_index]
    group_index = own_request // block_devices
    local_pages = jnp.concatenate([key_cache, value_cache], axis=2).reshape(
        page_local * page_rows, 2 * features
    )
    all_pages = lax.all_gather(local_pages, "seq", axis=0, tiled=False).reshape(
        seq_count * page_local, page_rows, 2 * features
    )
    extra = jnp.zeros((row_count, 128), jnp.bfloat16)
    extra = extra.at[:, 0:TOPK].set(routes.astype(jnp.bfloat16))
    extra = extra.at[:, TOPK].set(lengths[0].astype(jnp.bfloat16))
    packed = jnp.concatenate([queries, suffix_keys, suffix_values, hidden, extra], axis=1)
    pieces = packed.reshape(seq_count, row_count // seq_count, packed.shape[1])
    spread = lax.all_to_all(pieces, "seq", split_axis=0, concat_axis=0, tiled=True)
    spread = jnp.take(spread, inverse_destination, axis=0)
    moved = lax.all_to_all(spread, "seq", split_axis=0, concat_axis=0, tiled=True).reshape(
        row_count, packed.shape[1]
    )
    queries = moved[:, 0:features]
    suffix_keys = moved[:, features : 2 * features]
    suffix_values = moved[:, 2 * features : 3 * features]
    hidden = moved[:, 3 * features : 3 * features + column_width]
    tail = 3 * features + column_width
    routes = moved[:, tail : tail + TOPK].astype(jnp.int32)
    length = moved[0, tail + TOPK].astype(jnp.int32)
    chosen = lax.dynamic_slice_in_dim(inverse, group_index * group_pages, group_pages, 0)
    held_pages = jnp.take(all_pages, chosen, axis=0)
    prefix_keys = held_pages[:, :, :features].reshape(group_pages * page_rows, features)
    prefix_values = held_pages[:, :, features:].reshape(group_pages * page_rows, features)
    attended = attend_rows(
        queries, suffix_keys, suffix_values, prefix_keys, prefix_values, length, local_heads
    )
    stacked = jnp.concatenate([attended, hidden, router_weight.T], axis=0)
    gathered = lax.all_gather(stacked, "head", axis=1, tiled=True)
    full_attended = gathered[:row_count]
    full_hidden = gathered[row_count : 2 * row_count]
    full_router = gathered[2 * row_count :].T
    full_weight = lax.all_gather(out_weight, "head", axis=0, tiled=True)
    resid = full_hidden.astype(jnp.float32) + jnp.dot(
        full_attended, full_weight, preferred_element_type=jnp.float32
    )
    normed = (
        resid * lax.rsqrt(jnp.mean(resid * resid, axis=1, keepdims=True) + norm_eps) * norm_gain
    ).astype(jnp.bfloat16)
    logits = jnp.dot(normed, full_router, preferred_element_type=jnp.float32)
    chosen_logits = jnp.take_along_axis(logits, routes, axis=1)
    gate_first = jax.nn.sigmoid(chosen_logits[:, 0] - chosen_logits[:, 1])
    gate_second = jax.nn.sigmoid(chosen_logits[:, 1] - chosen_logits[:, 0])
    target_device, local_slot, slot_rank = slot_table(routes, replicas, per_device, EXPERTS)
    slot_flat = (target_device * per_device + local_slot) * capacity + slot_rank
    slot_total = seq_count * per_device * capacity
    pair_count = row_count * TOPK
    slot_pair = (
        jnp.zeros((slot_total,), jnp.int32)
        .at[slot_flat]
        .set(jnp.arange(pair_count, dtype=jnp.int32), mode="drop")
    )
    send_rows = jnp.take(normed, slot_pair // TOPK, axis=0).reshape(
        seq_count, per_device, capacity, normed.shape[1]
    )
    slots = lax.all_to_all(send_rows, "seq", split_axis=0, concat_axis=0, tiled=True)
    gate_act = jnp.einsum("spnd,pdf->spnf", slots, gate_weight, preferred_element_type=jnp.float32)
    up_act = jnp.einsum("spnd,pdf->spnf", slots, up_weight, preferred_element_type=jnp.float32)
    expert_hidden = (jax.nn.gelu(gate_act, approximate=True) * up_act).astype(jnp.bfloat16)
    partial_out = jnp.einsum(
        "spnf,pdf->spnd", expert_hidden, down_weight, preferred_element_type=jnp.float32
    )
    part_dims = partial_out.shape
    split_part = partial_out.reshape(
        part_dims[0], part_dims[1], part_dims[2], head_count, part_dims[3] // head_count
    ).astype(jnp.bfloat16)
    by_head = lax.all_to_all(split_part, "head", split_axis=3, concat_axis=3, tiled=True)
    summed = jnp.sum(by_head.astype(jnp.float32), axis=3).astype(jnp.bfloat16)
    returned = lax.all_to_all(summed, "seq", split_axis=0, concat_axis=0, tiled=True)
    picked = (
        returned[target_device, local_slot, slot_rank]
        .astype(jnp.float32)
        .reshape(row_count, TOPK, column_width)
    )
    resid_columns = lax.dynamic_slice_in_dim(resid, head_index * column_width, column_width, 1)
    layer = resid_columns + gate_first[:, None] * picked[:, 0] + gate_second[:, None] * picked[:, 1]
    layer = layer.astype(jnp.bfloat16)
    live_rows = jnp.arange(row_count, dtype=jnp.int32) < length
    return jnp.where(live_rows[:, None], layer, jnp.zeros_like(layer))


def solution(mesh):
    return jax.shard_map(
        on_device,
        mesh=mesh,
        in_specs=(
            P("seq", "head"),
            P("seq", "head"),
            P("seq", "head"),
            P("seq", "head"),
            P("seq"),
            P("seq", None, "head"),
            P("seq", None, "head"),
            P(),
            P("head", None),
            P(),
            P("head", None),
            P("seq", None),
            P("seq", None, "head"),
            P("seq", None, "head"),
            P("seq", None, "head"),
            P(),
        ),
        out_specs=P("seq", "head"),
        check_vma=False,
    )
```

```python
import jax
import jax.numpy as jnp
from jax import lax
from jax.sharding import Mesh, PartitionSpec as P

DH = 64
EXPERTS = 16
TOPK = 2
GROUPS = 4


norm_eps = 1e-06


def page_inverse(page_group, group_pages, groups):
    page_total = page_group.shape[0]
    onehot = (page_group[:, None] == jnp.arange(groups, dtype=jnp.int32)[None, :]).astype(jnp.int32)
    page_rank = jnp.sum((jnp.cumsum(onehot, axis=0) - 1) * onehot, axis=1)
    target = page_group * group_pages + page_rank
    return (
        jnp.zeros((page_total,), jnp.int32).at[target].set(jnp.arange(page_total, dtype=jnp.int32))
    )


def attend_rows(query_rows, key_rows, value_rows, prefix_keys, prefix_values, length, head_total):
    row_count = query_rows.shape[0]
    head_size = query_rows.shape[1] // head_total
    scale = head_size ** (-0.5)

    def heads_of(array):
        return array.reshape(array.shape[0], head_total, head_size)

    prefix_scores = (
        jnp.einsum(
            "qhd,khd->hqk",
            heads_of(query_rows),
            heads_of(prefix_keys),
            preferred_element_type=jnp.float32,
        )
        * scale
    )
    suffix_scores = (
        jnp.einsum(
            "qhd,khd->hqk",
            heads_of(query_rows),
            heads_of(key_rows),
            preferred_element_type=jnp.float32,
        )
        * scale
    )
    query_pos = jnp.arange(row_count, dtype=jnp.int32)[:, None]
    key_pos = jnp.arange(row_count, dtype=jnp.int32)[None, :]
    allowed = (key_pos <= query_pos) & (key_pos < length)
    suffix_scores = jnp.where(allowed[None], suffix_scores, -jnp.inf)
    row_max = jnp.maximum(jnp.max(prefix_scores, axis=2), jnp.max(suffix_scores, axis=2))[..., None]
    prefix_exp = jnp.exp(prefix_scores - row_max)
    suffix_exp = jnp.exp(suffix_scores - row_max)
    denominators = jnp.sum(prefix_exp, axis=2, keepdims=True) + jnp.sum(
        suffix_exp, axis=2, keepdims=True
    )
    prefix_probs = (prefix_exp / denominators).astype(jnp.bfloat16)
    suffix_probs = (suffix_exp / denominators).astype(jnp.bfloat16)
    mixed_heads = jnp.einsum(
        "hqk,khd->qhd", prefix_probs, heads_of(prefix_values), preferred_element_type=jnp.float32
    )
    mixed_heads = mixed_heads + jnp.einsum(
        "hqk,khd->qhd", suffix_probs, heads_of(value_rows), preferred_element_type=jnp.float32
    )
    return mixed_heads.reshape(row_count, head_total * head_size).astype(jnp.bfloat16)


def slot_table(route_rows, replicas, per_device, experts):
    row_count, topk_count = route_rows.shape
    sub_rows = row_count // replicas
    flat_routes = route_rows.reshape(replicas, sub_rows * topk_count)
    onehot = (flat_routes[..., None] == jnp.arange(experts, dtype=jnp.int32)).astype(jnp.int32)
    slot_rank = jnp.sum((jnp.cumsum(onehot, axis=1) - 1) * onehot, axis=2).reshape(-1)
    expert_flat = route_rows.reshape(-1)
    block_of = jnp.arange(row_count * topk_count, dtype=jnp.int32) // (sub_rows * topk_count)
    target_device = expert_flat // per_device * replicas + block_of
    local_slot = expert_flat % per_device
    return (target_device, local_slot, slot_rank)


def on_device(
    hidden,
    queries,
    suffix_keys,
    suffix_values,
    lengths,
    key_cache,
    value_cache,
    page_group,
    out_weight,
    norm_gain,
    router_weight,
    routes,
    gate_weight,
    up_weight,
    down_weight,
    destinations,
):
    expert_count = lax.axis_size("ex")
    replica_count = lax.axis_size("rep")
    seq_count = expert_count * replica_count
    head_count = lax.axis_size("head")
    seq_index = lax.axis_index("ex") * replica_count + lax.axis_index("rep")
    head_index = lax.axis_index("head")
    row_count = hidden.shape[0]
    column_width = hidden.shape[1]
    features = queries.shape[1]
    local_heads = features // DH
    block_devices = seq_count // GROUPS
    page_local = key_cache.shape[0]
    page_rows = key_cache.shape[1]
    group_pages = page_local * block_devices
    capacity = row_count * TOPK // expert_count
    ring = [
        lax.ppermute(
            out_weight,
            "head",
            [(source, (source + shift) % head_count) for source in range(head_count)],
        )
        for shift in range(1, head_count)
    ]
    rotated_weight = jnp.concatenate([out_weight] + ring, axis=0)
    inverse = page_inverse(page_group, group_pages, GROUPS)
    inverse_destination = (
        jnp.zeros((seq_count,), jnp.int32)
        .at[destinations]
        .set(jnp.arange(seq_count, dtype=jnp.int32))
    )
    own_request = inverse_destination[seq_index]
    group_index = own_request // block_devices
    local_pages = jnp.concatenate([key_cache, value_cache], axis=2).reshape(
        page_local * page_rows, 2 * features
    )
    all_pages = lax.all_gather(local_pages, SEQ, axis=0, tiled=False).reshape(
        seq_count * page_local, page_rows, 2 * features
    )
    extra = jnp.zeros((row_count, 128), jnp.bfloat16)
    extra = extra.at[:, 0:TOPK].set(routes.astype(jnp.bfloat16))
    extra = extra.at[:, TOPK].set(lengths[0].astype(jnp.bfloat16))
    packed = jnp.concatenate([queries, suffix_keys, suffix_values, hidden, extra], axis=1)
    pieces = packed.reshape(seq_count, row_count // seq_count, packed.shape[1])
    spread = lax.all_to_all(pieces, SEQ, split_axis=0, concat_axis=0, tiled=True)
    spread = jnp.take(spread, inverse_destination, axis=0)
    moved = lax.all_to_all(spread, SEQ, split_axis=0, concat_axis=0, tiled=True).reshape(
        row_count, packed.shape[1]
    )
    queries = moved[:, 0:features]
    suffix_keys = moved[:, features : 2 * features]
    suffix_values = moved[:, 2 * features : 3 * features]
    hidden = moved[:, 3 * features : 3 * features + column_width]
    tail = 3 * features + column_width
    routes = moved[:, tail : tail + TOPK].astype(jnp.int32)
    length = moved[0, tail + TOPK].astype(jnp.int32)
    chosen = lax.dynamic_slice_in_dim(inverse, group_index * group_pages, group_pages, 0)
    held_pages = jnp.take(all_pages, chosen, axis=0)
    prefix_keys = held_pages[:, :, :features].reshape(group_pages * page_rows, features)
    prefix_values = held_pages[:, :, features:].reshape(group_pages * page_rows, features)
    attended = attend_rows(
        queries, suffix_keys, suffix_values, prefix_keys, prefix_values, length, local_heads
    )
    stacked = jnp.concatenate([attended, hidden, router_weight.T], axis=0)
    gathered = lax.all_gather(stacked, "head", axis=1, tiled=True)
    full_attended = gathered[:row_count]
    full_hidden = gathered[row_count : 2 * row_count]
    full_router = gathered[2 * row_count :].T
    source_head = (head_index - jnp.arange(head_count, dtype=jnp.int32)) % head_count
    rotated_attended = jnp.take(
        full_attended.reshape(row_count, head_count, features), source_head, axis=1
    ).reshape(row_count, head_count * features)
    resid = full_hidden.astype(jnp.float32) + jnp.dot(
        rotated_attended, rotated_weight, preferred_element_type=jnp.float32
    )
    normed = (
        resid * lax.rsqrt(jnp.mean(resid * resid, axis=1, keepdims=True) + norm_eps) * norm_gain
    ).astype(jnp.bfloat16)
    logits = jnp.dot(normed, full_router, preferred_element_type=jnp.float32)
    chosen_logits = jnp.take_along_axis(logits, routes, axis=1)
    gate_first = jax.nn.sigmoid(chosen_logits[:, 0] - chosen_logits[:, 1])
    gate_second = jax.nn.sigmoid(chosen_logits[:, 1] - chosen_logits[:, 0])
    pair_count = row_count * TOPK
    expert_flat = routes.reshape(-1)
    onehot = (expert_flat[:, None] == jnp.arange(expert_count, dtype=jnp.int32)).astype(jnp.int32)
    slot_rank = jnp.sum((jnp.cumsum(onehot, axis=0) - 1) * onehot, axis=1)
    slot_flat = expert_flat * capacity + slot_rank
    slot_pair = (
        jnp.zeros((expert_count * capacity,), jnp.int32)
        .at[slot_flat]
        .set(jnp.arange(pair_count, dtype=jnp.int32), mode="drop")
    )
    send_rows = jnp.take(normed, slot_pair // TOPK, axis=0).reshape(
        expert_count, capacity, normed.shape[1]
    )
    slots = lax.all_to_all(send_rows, "ex", split_axis=0, concat_axis=0, tiled=True)
    gate_act = jnp.einsum("snd,df->snf", slots, gate_weight[0], preferred_element_type=jnp.float32)
    up_act = jnp.einsum("snd,df->snf", slots, up_weight[0], preferred_element_type=jnp.float32)
    expert_hidden = (jax.nn.gelu(gate_act, approximate=True) * up_act).astype(jnp.bfloat16)
    partial_out = jnp.einsum(
        "snf,df->snd", expert_hidden, down_weight[0], preferred_element_type=jnp.float32
    )
    split_part = partial_out.reshape(
        expert_count, capacity, head_count, column_width
    ).astype(jnp.bfloat16)
    by_head = lax.all_to_all(split_part, "head", split_axis=2, concat_axis=2, tiled=True)
    summed = jnp.sum(by_head.astype(jnp.float32), axis=2).astype(jnp.bfloat16)
    returned = lax.all_to_all(summed, "ex", split_axis=0, concat_axis=0, tiled=True)
    picked = (
        returned[expert_flat, slot_rank].astype(jnp.float32).reshape(row_count, TOPK, column_width)
    )
    resid_columns = lax.dynamic_slice_in_dim(resid, head_index * column_width, column_width, 1)
    layer = resid_columns + gate_first[:, None] * picked[:, 0] + gate_second[:, None] * picked[:, 1]
    layer = layer.astype(jnp.bfloat16)
    live_rows = jnp.arange(row_count, dtype=jnp.int32) < length
    return jnp.where(live_rows[:, None], layer, jnp.zeros_like(layer))


SEQ = ("ex", "rep")


def solution(mesh):
    seq_count = mesh.shape["seq"]
    fine = Mesh(
        mesh.devices.reshape(EXPERTS, seq_count // EXPERTS, mesh.shape["head"]),
        ("ex", "rep", "head"),
    )
    return jax.shard_map(
        on_device,
        mesh=fine,
        in_specs=(
            P(SEQ, "head"),
            P(SEQ, "head"),
            P(SEQ, "head"),
            P(SEQ, "head"),
            P(SEQ),
            P(SEQ, None, "head"),
            P(SEQ, None, "head"),
            P(),
            P("head", None),
            P(),
            P("head", None),
            P(SEQ, None),
            P(SEQ, None, "head"),
            P(SEQ, None, "head"),
            P(SEQ, None, "head"),
            P(),
        ),
        out_specs=P(SEQ, "head"),
        check_vma=False,
    )
```

```python
import jax
import jax.numpy as jnp
from jax import lax
from jax.sharding import Mesh, PartitionSpec as P

DH = 64
EXPERTS = 16
TOPK = 2
GROUPS = 4


norm_eps = 1e-06


def page_inverse(page_group, group_pages, groups):
    page_total = page_group.shape[0]
    onehot = (page_group[:, None] == jnp.arange(groups, dtype=jnp.int32)[None, :]).astype(jnp.int32)
    page_rank = jnp.sum((jnp.cumsum(onehot, axis=0) - 1) * onehot, axis=1)
    target = page_group * group_pages + page_rank
    return (
        jnp.zeros((page_total,), jnp.int32).at[target].set(jnp.arange(page_total, dtype=jnp.int32))
    )


def attend_rows(query_rows, key_rows, value_rows, prefix_keys, prefix_values, length, head_total):
    row_count = query_rows.shape[0]
    head_size = query_rows.shape[1] // head_total
    scale = head_size ** (-0.5)

    def heads_of(array):
        return array.reshape(array.shape[0], head_total, head_size)

    prefix_scores = (
        jnp.einsum(
            "qhd,khd->hqk",
            heads_of(query_rows),
            heads_of(prefix_keys),
            preferred_element_type=jnp.float32,
        )
        * scale
    )
    suffix_scores = (
        jnp.einsum(
            "qhd,khd->hqk",
            heads_of(query_rows),
            heads_of(key_rows),
            preferred_element_type=jnp.float32,
        )
        * scale
    )
    query_pos = jnp.arange(row_count, dtype=jnp.int32)[:, None]
    key_pos = jnp.arange(row_count, dtype=jnp.int32)[None, :]
    allowed = (key_pos <= query_pos) & (key_pos < length)
    suffix_scores = jnp.where(allowed[None], suffix_scores, -jnp.inf)
    row_max = jnp.maximum(jnp.max(prefix_scores, axis=2), jnp.max(suffix_scores, axis=2))[..., None]
    prefix_exp = jnp.exp(prefix_scores - row_max)
    suffix_exp = jnp.exp(suffix_scores - row_max)
    denominators = jnp.sum(prefix_exp, axis=2, keepdims=True) + jnp.sum(
        suffix_exp, axis=2, keepdims=True
    )
    prefix_probs = (prefix_exp / denominators).astype(jnp.bfloat16)
    suffix_probs = (suffix_exp / denominators).astype(jnp.bfloat16)
    mixed_heads = jnp.einsum(
        "hqk,khd->qhd", prefix_probs, heads_of(prefix_values), preferred_element_type=jnp.float32
    )
    mixed_heads = mixed_heads + jnp.einsum(
        "hqk,khd->qhd", suffix_probs, heads_of(value_rows), preferred_element_type=jnp.float32
    )
    return mixed_heads.reshape(row_count, head_total * head_size).astype(jnp.bfloat16)


def slot_table(route_rows, replicas, per_device, experts):
    row_count, topk_count = route_rows.shape
    sub_rows = row_count // replicas
    flat_routes = route_rows.reshape(replicas, sub_rows * topk_count)
    onehot = (flat_routes[..., None] == jnp.arange(experts, dtype=jnp.int32)).astype(jnp.int32)
    slot_rank = jnp.sum((jnp.cumsum(onehot, axis=1) - 1) * onehot, axis=2).reshape(-1)
    expert_flat = route_rows.reshape(-1)
    block_of = jnp.arange(row_count * topk_count, dtype=jnp.int32) // (sub_rows * topk_count)
    target_device = expert_flat // per_device * replicas + block_of
    local_slot = expert_flat % per_device
    return (target_device, local_slot, slot_rank)


def on_device(
    hidden,
    queries,
    suffix_keys,
    suffix_values,
    lengths,
    key_cache,
    value_cache,
    page_group,
    out_weight,
    norm_gain,
    router_weight,
    routes,
    gate_weight,
    up_weight,
    down_weight,
    destinations,
):
    expert_count = lax.axis_size("ex")
    replica_count = lax.axis_size("rep")
    seq_count = expert_count * replica_count
    head_count = lax.axis_size("head")
    seq_index = lax.axis_index("ex") * replica_count + lax.axis_index("rep")
    head_index = lax.axis_index("head")
    row_count = hidden.shape[0]
    column_width = hidden.shape[1]
    features = queries.shape[1]
    local_heads = features // DH
    block_devices = seq_count // GROUPS
    page_local = key_cache.shape[0]
    page_rows = key_cache.shape[1]
    group_pages = page_local * block_devices
    capacity = row_count * TOPK // expert_count
    def head_ring(block):
        return [
            lax.ppermute(
                block,
                "head",
                [(source, (source + shift) % head_count) for source in range(head_count)],
            )
            for shift in range(1, head_count)
        ]

    rotated_weight = jnp.concatenate([out_weight] + head_ring(out_weight), axis=0)
    inverse = page_inverse(page_group, group_pages, GROUPS)
    inverse_destination = (
        jnp.zeros((seq_count,), jnp.int32)
        .at[destinations]
        .set(jnp.arange(seq_count, dtype=jnp.int32))
    )
    own_request = inverse_destination[seq_index]
    group_index = own_request // block_devices
    local_pages = jnp.concatenate([key_cache, value_cache], axis=2).reshape(
        page_local * page_rows, 2 * features
    )
    all_pages = lax.all_gather(local_pages, SEQ, axis=0, tiled=False).reshape(
        seq_count * page_local, page_rows, 2 * features
    )
    extra = jnp.zeros((row_count, 128), jnp.bfloat16)
    extra = extra.at[:, 0:TOPK].set(routes.astype(jnp.bfloat16))
    extra = extra.at[:, TOPK].set(lengths[0].astype(jnp.bfloat16))
    packed = jnp.concatenate([queries, suffix_keys, suffix_values, hidden, extra], axis=1)
    pieces = packed.reshape(seq_count, row_count // seq_count, packed.shape[1])
    spread = lax.all_to_all(pieces, SEQ, split_axis=0, concat_axis=0, tiled=True)
    spread = jnp.take(spread, inverse_destination, axis=0)
    moved = lax.all_to_all(spread, SEQ, split_axis=0, concat_axis=0, tiled=True).reshape(
        row_count, packed.shape[1]
    )
    queries = moved[:, 0:features]
    suffix_keys = moved[:, features : 2 * features]
    suffix_values = moved[:, 2 * features : 3 * features]
    hidden = moved[:, 3 * features : 3 * features + column_width]
    tail = 3 * features + column_width
    routes = moved[:, tail : tail + TOPK].astype(jnp.int32)
    length = moved[0, tail + TOPK].astype(jnp.int32)
    chosen = lax.dynamic_slice_in_dim(inverse, group_index * group_pages, group_pages, 0)
    held_pages = jnp.take(all_pages, chosen, axis=0)
    prefix_keys = held_pages[:, :, :features].reshape(group_pages * page_rows, features)
    prefix_values = held_pages[:, :, features:].reshape(group_pages * page_rows, features)
    attended = attend_rows(
        queries, suffix_keys, suffix_values, prefix_keys, prefix_values, length, local_heads
    )
    side = jnp.concatenate([hidden, router_weight.T], axis=0)
    rotated_side = jnp.stack([side] + head_ring(side), axis=0)
    source_head = (head_index - jnp.arange(head_count, dtype=jnp.int32)) % head_count
    side_blocks = jnp.take(rotated_side, source_head, axis=0)
    full_side = jnp.transpose(side_blocks, (1, 0, 2)).reshape(side.shape[0], head_count * features)
    full_hidden = full_side[:row_count]
    full_router = full_side[row_count:].T
    rotated_attended = jnp.concatenate([attended] + head_ring(attended), axis=1)
    resid = full_hidden.astype(jnp.float32) + jnp.dot(
        rotated_attended, rotated_weight, preferred_element_type=jnp.float32
    )
    normed = (
        resid * lax.rsqrt(jnp.mean(resid * resid, axis=1, keepdims=True) + norm_eps) * norm_gain
    ).astype(jnp.bfloat16)
    logits = jnp.dot(normed, full_router, preferred_element_type=jnp.float32)
    chosen_logits = jnp.take_along_axis(logits, routes, axis=1)
    gate_first = jax.nn.sigmoid(chosen_logits[:, 0] - chosen_logits[:, 1])
    gate_second = jax.nn.sigmoid(chosen_logits[:, 1] - chosen_logits[:, 0])
    pair_count = row_count * TOPK
    expert_flat = routes.reshape(-1)
    onehot = (expert_flat[:, None] == jnp.arange(expert_count, dtype=jnp.int32)).astype(jnp.int32)
    slot_rank = jnp.sum((jnp.cumsum(onehot, axis=0) - 1) * onehot, axis=1)
    slot_flat = expert_flat * capacity + slot_rank
    slot_pair = (
        jnp.zeros((expert_count * capacity,), jnp.int32)
        .at[slot_flat]
        .set(jnp.arange(pair_count, dtype=jnp.int32), mode="drop")
    )
    send_rows = jnp.take(normed, slot_pair // TOPK, axis=0).reshape(
        expert_count, capacity, normed.shape[1]
    )
    slots = lax.all_to_all(send_rows, "ex", split_axis=0, concat_axis=0, tiled=True)
    gate_act = jnp.einsum("snd,df->snf", slots, gate_weight[0], preferred_element_type=jnp.float32)
    up_act = jnp.einsum("snd,df->snf", slots, up_weight[0], preferred_element_type=jnp.float32)
    expert_hidden = (jax.nn.gelu(gate_act, approximate=True) * up_act).astype(jnp.bfloat16)
    partial_out = jnp.einsum(
        "snf,df->snd", expert_hidden, down_weight[0], preferred_element_type=jnp.float32
    )
    split_part = jnp.transpose(
        partial_out.reshape(expert_count, capacity, head_count, column_width), (0, 2, 1, 3)
    ).astype(jnp.bfloat16)
    split_part = split_part.reshape(expert_count * head_count, capacity, column_width)
    arrived = lax.all_to_all(split_part, ("ex", "head"), split_axis=0, concat_axis=0, tiled=True)
    arrived = arrived.reshape(expert_count, head_count, capacity, column_width)
    returned = jnp.sum(arrived.astype(jnp.float32), axis=1).astype(jnp.bfloat16)
    picked = (
        returned[expert_flat, slot_rank].astype(jnp.float32).reshape(row_count, TOPK, column_width)
    )
    resid_columns = lax.dynamic_slice_in_dim(resid, head_index * column_width, column_width, 1)
    layer = resid_columns + gate_first[:, None] * picked[:, 0] + gate_second[:, None] * picked[:, 1]
    layer = layer.astype(jnp.bfloat16)
    live_rows = jnp.arange(row_count, dtype=jnp.int32) < length
    return jnp.where(live_rows[:, None], layer, jnp.zeros_like(layer))


SEQ = ("ex", "rep")


def solution(mesh):
    seq_count = mesh.shape["seq"]
    fine = Mesh(
        mesh.devices.reshape(EXPERTS, seq_count // EXPERTS, mesh.shape["head"]),
        ("ex", "rep", "head"),
    )
    return jax.shard_map(
        on_device,
        mesh=fine,
        in_specs=(
            P(SEQ, "head"),
            P(SEQ, "head"),
            P(SEQ, "head"),
            P(SEQ, "head"),
            P(SEQ),
            P(SEQ, None, "head"),
            P(SEQ, None, "head"),
            P(),
            P("head", None),
            P(),
            P("head", None),
            P(SEQ, None),
            P(SEQ, None, "head"),
            P(SEQ, None, "head"),
            P(SEQ, None, "head"),
            P(),
        ),
        out_specs=P(SEQ, "head"),
        check_vma=False,
    )
```

```python
import jax
import jax.numpy as jnp
from jax import lax
from jax.sharding import Mesh, PartitionSpec as P

DH = 64
EXPERTS = 16
TOPK = 2
GROUPS = 4


norm_eps = 1e-06


def page_inverse(page_group, group_pages, groups):
    page_total = page_group.shape[0]
    onehot = (page_group[:, None] == jnp.arange(groups, dtype=jnp.int32)[None, :]).astype(jnp.int32)
    page_rank = jnp.sum((jnp.cumsum(onehot, axis=0) - 1) * onehot, axis=1)
    target = page_group * group_pages + page_rank
    return (
        jnp.zeros((page_total,), jnp.int32).at[target].set(jnp.arange(page_total, dtype=jnp.int32))
    )


def attend_rows(query_rows, key_rows, value_rows, prefix_keys, prefix_values, length, head_total):
    row_count = query_rows.shape[0]
    head_size = query_rows.shape[1] // head_total
    scale = head_size ** (-0.5)

    def heads_of(array):
        return array.reshape(array.shape[0], head_total, head_size)

    prefix_scores = (
        jnp.einsum(
            "qhd,khd->hqk",
            heads_of(query_rows),
            heads_of(prefix_keys),
            preferred_element_type=jnp.float32,
        )
        * scale
    )
    suffix_scores = (
        jnp.einsum(
            "qhd,khd->hqk",
            heads_of(query_rows),
            heads_of(key_rows),
            preferred_element_type=jnp.float32,
        )
        * scale
    )
    query_pos = jnp.arange(row_count, dtype=jnp.int32)[:, None]
    key_pos = jnp.arange(row_count, dtype=jnp.int32)[None, :]
    allowed = (key_pos <= query_pos) & (key_pos < length)
    suffix_scores = jnp.where(allowed[None], suffix_scores, -jnp.inf)
    row_max = jnp.maximum(jnp.max(prefix_scores, axis=2), jnp.max(suffix_scores, axis=2))[..., None]
    prefix_exp = jnp.exp(prefix_scores - row_max)
    suffix_exp = jnp.exp(suffix_scores - row_max)
    denominators = jnp.sum(prefix_exp, axis=2, keepdims=True) + jnp.sum(
        suffix_exp, axis=2, keepdims=True
    )
    prefix_probs = (prefix_exp / denominators).astype(jnp.bfloat16)
    suffix_probs = (suffix_exp / denominators).astype(jnp.bfloat16)
    mixed_heads = jnp.einsum(
        "hqk,khd->qhd", prefix_probs, heads_of(prefix_values), preferred_element_type=jnp.float32
    )
    mixed_heads = mixed_heads + jnp.einsum(
        "hqk,khd->qhd", suffix_probs, heads_of(value_rows), preferred_element_type=jnp.float32
    )
    return mixed_heads.reshape(row_count, head_total * head_size).astype(jnp.bfloat16)


def slot_table(route_rows, replicas, per_device, experts):
    row_count, topk_count = route_rows.shape
    sub_rows = row_count // replicas
    flat_routes = route_rows.reshape(replicas, sub_rows * topk_count)
    onehot = (flat_routes[..., None] == jnp.arange(experts, dtype=jnp.int32)).astype(jnp.int32)
    slot_rank = jnp.sum((jnp.cumsum(onehot, axis=1) - 1) * onehot, axis=2).reshape(-1)
    expert_flat = route_rows.reshape(-1)
    block_of = jnp.arange(row_count * topk_count, dtype=jnp.int32) // (sub_rows * topk_count)
    target_device = expert_flat // per_device * replicas + block_of
    local_slot = expert_flat % per_device
    return (target_device, local_slot, slot_rank)


def on_device(
    hidden,
    queries,
    suffix_keys,
    suffix_values,
    lengths,
    key_cache,
    value_cache,
    page_group,
    out_weight,
    norm_gain,
    router_weight,
    routes,
    gate_weight,
    up_weight,
    down_weight,
    destinations,
):
    expert_count = lax.axis_size("ex")
    replica_count = lax.axis_size("rep")
    seq_count = expert_count * replica_count
    head_count = lax.axis_size("head")
    seq_index = lax.axis_index("ex") * replica_count + lax.axis_index("rep")
    head_index = lax.axis_index("head")
    row_count = hidden.shape[0]
    column_width = hidden.shape[1]
    features = queries.shape[1]
    local_heads = features // DH
    block_devices = seq_count // GROUPS
    page_local = key_cache.shape[0]
    page_rows = key_cache.shape[1]
    group_pages = page_local * block_devices
    capacity = row_count * TOPK // expert_count
    def head_ring(block):
        return [
            lax.ppermute(
                block,
                "head",
                [(source, (source + shift) % head_count) for source in range(head_count)],
            )
            for shift in range(1, head_count)
        ]

    rotated_weight = jnp.concatenate([out_weight] + head_ring(out_weight), axis=0)
    inverse = page_inverse(page_group, group_pages, GROUPS)
    inverse_destination = (
        jnp.zeros((seq_count,), jnp.int32)
        .at[destinations]
        .set(jnp.arange(seq_count, dtype=jnp.int32))
    )
    own_request = inverse_destination[seq_index]
    group_index = own_request // block_devices
    local_pages = jnp.concatenate([key_cache, value_cache], axis=2).reshape(
        page_local * page_rows, 2 * features
    )
    all_pages = lax.all_gather(local_pages, SEQ, axis=0, tiled=False).reshape(
        seq_count * page_local, page_rows, 2 * features
    )
    extra = jnp.zeros((row_count, 128), jnp.bfloat16)
    extra = extra.at[:, 0:TOPK].set(routes.astype(jnp.bfloat16))
    extra = extra.at[:, TOPK].set(lengths[0].astype(jnp.bfloat16))
    packed = jnp.concatenate([queries, suffix_keys, suffix_values, hidden, extra], axis=1)
    pieces = packed.reshape(seq_count, row_count // seq_count, packed.shape[1])
    spread = lax.all_to_all(pieces, SEQ, split_axis=0, concat_axis=0, tiled=True)
    spread = jnp.take(spread, inverse_destination, axis=0)
    moved = lax.all_to_all(spread, SEQ, split_axis=0, concat_axis=0, tiled=True).reshape(
        row_count, packed.shape[1]
    )
    queries = moved[:, 0:features]
    suffix_keys = moved[:, features : 2 * features]
    suffix_values = moved[:, 2 * features : 3 * features]
    hidden = moved[:, 3 * features : 3 * features + column_width]
    tail = 3 * features + column_width
    routes = moved[:, tail : tail + TOPK].astype(jnp.int32)
    length = moved[0, tail + TOPK].astype(jnp.int32)
    chosen = lax.dynamic_slice_in_dim(inverse, group_index * group_pages, group_pages, 0)
    held_pages = jnp.take(all_pages, chosen, axis=0)
    prefix_keys = held_pages[:, :, :features].reshape(group_pages * page_rows, features)
    prefix_values = held_pages[:, :, features:].reshape(group_pages * page_rows, features)
    attended = attend_rows(
        queries, suffix_keys, suffix_values, prefix_keys, prefix_values, length, local_heads
    )
    side = jnp.concatenate([hidden, router_weight.T], axis=0)
    rotated_side = jnp.stack([side] + head_ring(side), axis=0)
    source_head = (head_index - jnp.arange(head_count, dtype=jnp.int32)) % head_count
    side_blocks = jnp.take(rotated_side, source_head, axis=0)
    full_side = jnp.transpose(side_blocks, (1, 0, 2)).reshape(side.shape[0], head_count * features)
    full_hidden = full_side[:row_count]
    full_router = full_side[row_count:].T
    spread_attended = jnp.broadcast_to(attended[None], (head_count,) + attended.shape)
    by_source = lax.all_to_all(spread_attended, "head", split_axis=0, concat_axis=0, tiled=True)
    rotated_attended = jnp.transpose(jnp.take(by_source, source_head, axis=0), (1, 0, 2)).reshape(
        row_count, head_count * features
    )
    resid = full_hidden.astype(jnp.float32) + jnp.dot(
        rotated_attended, rotated_weight, preferred_element_type=jnp.float32
    )
    normed = (
        resid * lax.rsqrt(jnp.mean(resid * resid, axis=1, keepdims=True) + norm_eps) * norm_gain
    ).astype(jnp.bfloat16)
    logits = jnp.dot(normed, full_router, preferred_element_type=jnp.float32)
    chosen_logits = jnp.take_along_axis(logits, routes, axis=1)
    gate_first = jax.nn.sigmoid(chosen_logits[:, 0] - chosen_logits[:, 1])
    gate_second = jax.nn.sigmoid(chosen_logits[:, 1] - chosen_logits[:, 0])
    pair_count = row_count * TOPK
    expert_flat = routes.reshape(-1)
    onehot = (expert_flat[:, None] == jnp.arange(expert_count, dtype=jnp.int32)).astype(jnp.int32)
    slot_rank = jnp.sum((jnp.cumsum(onehot, axis=0) - 1) * onehot, axis=1)
    slot_flat = expert_flat * capacity + slot_rank
    slot_pair = (
        jnp.zeros((expert_count * capacity,), jnp.int32)
        .at[slot_flat]
        .set(jnp.arange(pair_count, dtype=jnp.int32), mode="drop")
    )
    send_rows = jnp.take(normed, slot_pair // TOPK, axis=0).reshape(
        expert_count, capacity, normed.shape[1]
    )
    slots = lax.all_to_all(send_rows, "ex", split_axis=0, concat_axis=0, tiled=True)
    gate_act = jnp.einsum("snd,df->snf", slots, gate_weight[0], preferred_element_type=jnp.float32)
    up_act = jnp.einsum("snd,df->snf", slots, up_weight[0], preferred_element_type=jnp.float32)
    expert_hidden = (jax.nn.gelu(gate_act, approximate=True) * up_act).astype(jnp.bfloat16)
    partial_out = jnp.einsum(
        "snf,df->snd", expert_hidden, down_weight[0], preferred_element_type=jnp.float32
    )
    split_part = jnp.transpose(
        partial_out.reshape(expert_count, capacity, head_count, column_width), (0, 2, 1, 3)
    ).astype(jnp.bfloat16)
    split_part = split_part.reshape(expert_count * head_count, capacity, column_width)
    arrived = lax.all_to_all(split_part, ("ex", "head"), split_axis=0, concat_axis=0, tiled=True)
    arrived = arrived.reshape(expert_count, head_count, capacity, column_width)
    returned = jnp.sum(arrived.astype(jnp.float32), axis=1).astype(jnp.bfloat16)
    picked = (
        returned[expert_flat, slot_rank].astype(jnp.float32).reshape(row_count, TOPK, column_width)
    )
    resid_columns = lax.dynamic_slice_in_dim(resid, head_index * column_width, column_width, 1)
    layer = resid_columns + gate_first[:, None] * picked[:, 0] + gate_second[:, None] * picked[:, 1]
    layer = layer.astype(jnp.bfloat16)
    live_rows = jnp.arange(row_count, dtype=jnp.int32) < length
    return jnp.where(live_rows[:, None], layer, jnp.zeros_like(layer))


SEQ = ("ex", "rep")


def solution(mesh):
    seq_count = mesh.shape["seq"]
    fine = Mesh(
        mesh.devices.reshape(EXPERTS, seq_count // EXPERTS, mesh.shape["head"]),
        ("ex", "rep", "head"),
    )
    return jax.shard_map(
        on_device,
        mesh=fine,
        in_specs=(
            P(SEQ, "head"),
            P(SEQ, "head"),
            P(SEQ, "head"),
            P(SEQ, "head"),
            P(SEQ),
            P(SEQ, None, "head"),
            P(SEQ, None, "head"),
            P(),
            P("head", None),
            P(),
            P("head", None),
            P(SEQ, None),
            P(SEQ, None, "head"),
            P(SEQ, None, "head"),
            P(SEQ, None, "head"),
            P(),
        ),
        out_specs=P(SEQ, "head"),
        check_vma=False,
    )
```

```python
import jax
import jax.numpy as jnp
from jax import lax
from jax.sharding import Mesh, PartitionSpec as P

DH = 64
EXPERTS = 16
TOPK = 2
GROUPS = 4


norm_eps = 1e-06


def page_inverse(page_group, group_pages, groups):
    page_total = page_group.shape[0]
    onehot = (page_group[:, None] == jnp.arange(groups, dtype=jnp.int32)[None, :]).astype(jnp.int32)
    page_rank = jnp.sum((jnp.cumsum(onehot, axis=0) - 1) * onehot, axis=1)
    target = page_group * group_pages + page_rank
    return (
        jnp.zeros((page_total,), jnp.int32).at[target].set(jnp.arange(page_total, dtype=jnp.int32))
    )


def attend_rows(query_rows, key_rows, value_rows, prefix_keys, prefix_values, length, head_total):
    row_count = query_rows.shape[0]
    features = query_rows.shape[1]
    head_size = features // head_total
    scale = head_size ** (-0.5)
    head_of_column = jnp.arange(features, dtype=jnp.int32) // head_size
    own_head = head_of_column[None, :] == jnp.arange(head_total, dtype=jnp.int32)[:, None]
    masked_queries = jnp.where(
        own_head[:, None, :], query_rows[None], jnp.zeros_like(query_rows)[None]
    ).reshape(head_total * row_count, features)
    prefix_scores = (
        jnp.dot(masked_queries, prefix_keys.T, preferred_element_type=jnp.float32) * scale
    ).reshape(head_total, row_count, -1)
    suffix_scores = (
        jnp.dot(masked_queries, key_rows.T, preferred_element_type=jnp.float32) * scale
    ).reshape(head_total, row_count, -1)
    query_pos = jnp.arange(row_count, dtype=jnp.int32)[:, None]
    key_pos = jnp.arange(row_count, dtype=jnp.int32)[None, :]
    allowed = (key_pos <= query_pos) & (key_pos < length)
    suffix_scores = jnp.where(allowed[None], suffix_scores, -jnp.inf)
    row_max = jnp.maximum(jnp.max(prefix_scores, axis=2), jnp.max(suffix_scores, axis=2))[..., None]
    prefix_exp = jnp.exp(prefix_scores - row_max)
    suffix_exp = jnp.exp(suffix_scores - row_max)
    denominators = jnp.sum(prefix_exp, axis=2, keepdims=True) + jnp.sum(
        suffix_exp, axis=2, keepdims=True
    )
    prefix_probs = (prefix_exp / denominators).astype(jnp.bfloat16)
    suffix_probs = (suffix_exp / denominators).astype(jnp.bfloat16)
    mixed = jnp.dot(
        prefix_probs.reshape(head_total * row_count, -1),
        prefix_values,
        preferred_element_type=jnp.float32,
    ) + jnp.dot(
        suffix_probs.reshape(head_total * row_count, -1),
        value_rows,
        preferred_element_type=jnp.float32,
    )
    mixed = mixed.reshape(head_total, row_count, features)
    picked = jnp.where(own_head[:, None, :], mixed, jnp.zeros_like(mixed))
    return jnp.sum(picked, axis=0).astype(jnp.bfloat16)


def slot_table(route_rows, replicas, per_device, experts):
    row_count, topk_count = route_rows.shape
    sub_rows = row_count // replicas
    flat_routes = route_rows.reshape(replicas, sub_rows * topk_count)
    onehot = (flat_routes[..., None] == jnp.arange(experts, dtype=jnp.int32)).astype(jnp.int32)
    slot_rank = jnp.sum((jnp.cumsum(onehot, axis=1) - 1) * onehot, axis=2).reshape(-1)
    expert_flat = route_rows.reshape(-1)
    block_of = jnp.arange(row_count * topk_count, dtype=jnp.int32) // (sub_rows * topk_count)
    target_device = expert_flat // per_device * replicas + block_of
    local_slot = expert_flat % per_device
    return (target_device, local_slot, slot_rank)


def on_device(
    hidden,
    queries,
    suffix_keys,
    suffix_values,
    lengths,
    key_cache,
    value_cache,
    page_group,
    out_weight,
    norm_gain,
    router_weight,
    routes,
    gate_weight,
    up_weight,
    down_weight,
    destinations,
):
    expert_count = lax.axis_size("ex")
    replica_count = lax.axis_size("rep")
    seq_count = expert_count * replica_count
    head_count = lax.axis_size("head")
    seq_index = lax.axis_index("ex") * replica_count + lax.axis_index("rep")
    head_index = lax.axis_index("head")
    row_count = hidden.shape[0]
    column_width = hidden.shape[1]
    features = queries.shape[1]
    local_heads = features // DH
    block_devices = seq_count // GROUPS
    page_local = key_cache.shape[0]
    page_rows = key_cache.shape[1]
    group_pages = page_local * block_devices
    capacity = row_count * TOPK // expert_count
    def head_ring(block):
        return [
            lax.ppermute(
                block,
                "head",
                [(source, (source + shift) % head_count) for source in range(head_count)],
            )
            for shift in range(1, head_count)
        ]

    rotated_weight = jnp.concatenate([out_weight] + head_ring(out_weight), axis=0)
    inverse = page_inverse(page_group, group_pages, GROUPS)
    inverse_destination = (
        jnp.zeros((seq_count,), jnp.int32)
        .at[destinations]
        .set(jnp.arange(seq_count, dtype=jnp.int32))
    )
    own_request = inverse_destination[seq_index]
    group_index = own_request // block_devices
    local_pages = jnp.concatenate([key_cache, value_cache], axis=2).reshape(
        page_local * page_rows, 2 * features
    )
    all_pages = lax.all_gather(local_pages, SEQ, axis=0, tiled=False).reshape(
        seq_count * page_local, page_rows, 2 * features
    )
    extra = jnp.zeros((row_count, 128), jnp.bfloat16)
    extra = extra.at[:, 0:TOPK].set(routes.astype(jnp.bfloat16))
    extra = extra.at[:, TOPK].set(lengths[0].astype(jnp.bfloat16))
    packed = jnp.concatenate([queries, suffix_keys, suffix_values, hidden, extra], axis=1)
    pieces = packed.reshape(seq_count, row_count // seq_count, packed.shape[1])
    spread = lax.all_to_all(pieces, SEQ, split_axis=0, concat_axis=0, tiled=True)
    spread = jnp.take(spread, inverse_destination, axis=0)
    moved = lax.all_to_all(spread, SEQ, split_axis=0, concat_axis=0, tiled=True).reshape(
        row_count, packed.shape[1]
    )
    queries = moved[:, 0:features]
    suffix_keys = moved[:, features : 2 * features]
    suffix_values = moved[:, 2 * features : 3 * features]
    hidden = moved[:, 3 * features : 3 * features + column_width]
    tail = 3 * features + column_width
    routes = moved[:, tail : tail + TOPK].astype(jnp.int32)
    length = moved[0, tail + TOPK].astype(jnp.int32)
    chosen = lax.dynamic_slice_in_dim(inverse, group_index * group_pages, group_pages, 0)
    held_pages = jnp.take(all_pages, chosen, axis=0)
    prefix_keys = held_pages[:, :, :features].reshape(group_pages * page_rows, features)
    prefix_values = held_pages[:, :, features:].reshape(group_pages * page_rows, features)
    attended = attend_rows(
        queries, suffix_keys, suffix_values, prefix_keys, prefix_values, length, local_heads
    )
    side = jnp.concatenate([hidden, router_weight.T], axis=0)
    rotated_side = jnp.stack([side] + head_ring(side), axis=0)
    source_head = (head_index - jnp.arange(head_count, dtype=jnp.int32)) % head_count
    side_blocks = jnp.take(rotated_side, source_head, axis=0)
    full_side = jnp.transpose(side_blocks, (1, 0, 2)).reshape(side.shape[0], head_count * features)
    full_hidden = full_side[:row_count]
    full_router = full_side[row_count:].T
    spread_attended = jnp.broadcast_to(attended[None], (head_count,) + attended.shape)
    by_source = lax.all_to_all(spread_attended, "head", split_axis=0, concat_axis=0, tiled=True)
    rotated_attended = jnp.transpose(jnp.take(by_source, source_head, axis=0), (1, 0, 2)).reshape(
        row_count, head_count * features
    )
    resid = full_hidden.astype(jnp.float32) + jnp.dot(
        rotated_attended, rotated_weight, preferred_element_type=jnp.float32
    )
    normed = (
        resid * lax.rsqrt(jnp.mean(resid * resid, axis=1, keepdims=True) + norm_eps) * norm_gain
    ).astype(jnp.bfloat16)
    logits = jnp.dot(normed, full_router, preferred_element_type=jnp.float32)
    chosen_logits = jnp.take_along_axis(logits, routes, axis=1)
    gate_first = jax.nn.sigmoid(chosen_logits[:, 0] - chosen_logits[:, 1])
    gate_second = jax.nn.sigmoid(chosen_logits[:, 1] - chosen_logits[:, 0])
    pair_count = row_count * TOPK
    expert_flat = routes.reshape(-1)
    onehot = (expert_flat[:, None] == jnp.arange(expert_count, dtype=jnp.int32)).astype(jnp.int32)
    slot_rank = jnp.sum((jnp.cumsum(onehot, axis=0) - 1) * onehot, axis=1)
    slot_flat = expert_flat * capacity + slot_rank
    slot_pair = (
        jnp.zeros((expert_count * capacity,), jnp.int32)
        .at[slot_flat]
        .set(jnp.arange(pair_count, dtype=jnp.int32), mode="drop")
    )
    send_rows = jnp.take(normed, slot_pair // TOPK, axis=0).reshape(
        expert_count, capacity, normed.shape[1]
    )
    slots = lax.all_to_all(send_rows, "ex", split_axis=0, concat_axis=0, tiled=True)
    gate_act = jnp.einsum("snd,df->snf", slots, gate_weight[0], preferred_element_type=jnp.float32)
    up_act = jnp.einsum("snd,df->snf", slots, up_weight[0], preferred_element_type=jnp.float32)
    expert_hidden = (jax.nn.gelu(gate_act, approximate=True) * up_act).astype(jnp.bfloat16)
    partial_out = jnp.einsum(
        "snf,df->snd", expert_hidden, down_weight[0], preferred_element_type=jnp.float32
    )
    split_part = jnp.transpose(
        partial_out.reshape(expert_count, capacity, head_count, column_width), (0, 2, 1, 3)
    ).astype(jnp.bfloat16)
    split_part = split_part.reshape(expert_count * head_count, capacity, column_width)
    arrived = lax.all_to_all(split_part, ("ex", "head"), split_axis=0, concat_axis=0, tiled=True)
    arrived = arrived.reshape(expert_count, head_count, capacity, column_width)
    returned = jnp.sum(arrived.astype(jnp.float32), axis=1).astype(jnp.bfloat16)
    picked = (
        returned[expert_flat, slot_rank].astype(jnp.float32).reshape(row_count, TOPK, column_width)
    )
    resid_columns = lax.dynamic_slice_in_dim(resid, head_index * column_width, column_width, 1)
    layer = resid_columns + gate_first[:, None] * picked[:, 0] + gate_second[:, None] * picked[:, 1]
    layer = layer.astype(jnp.bfloat16)
    live_rows = jnp.arange(row_count, dtype=jnp.int32) < length
    return jnp.where(live_rows[:, None], layer, jnp.zeros_like(layer))


SEQ = ("ex", "rep")


def solution(mesh):
    seq_count = mesh.shape["seq"]
    fine = Mesh(
        mesh.devices.reshape(EXPERTS, seq_count // EXPERTS, mesh.shape["head"]),
        ("ex", "rep", "head"),
    )
    return jax.shard_map(
        on_device,
        mesh=fine,
        in_specs=(
            P(SEQ, "head"),
            P(SEQ, "head"),
            P(SEQ, "head"),
            P(SEQ, "head"),
            P(SEQ),
            P(SEQ, None, "head"),
            P(SEQ, None, "head"),
            P(),
            P("head", None),
            P(),
            P("head", None),
            P(SEQ, None),
            P(SEQ, None, "head"),
            P(SEQ, None, "head"),
            P(SEQ, None, "head"),
            P(),
        ),
        out_specs=P(SEQ, "head"),
        check_vma=False,
    )
```

```python
import jax
import jax.numpy as jnp
from jax import lax
from jax.sharding import Mesh, PartitionSpec as P

DH = 64
EXPERTS = 16
TOPK = 2
GROUPS = 4


norm_eps = 1e-06


def page_inverse(page_group, group_pages, groups):
    page_total = page_group.shape[0]
    onehot = (page_group[:, None] == jnp.arange(groups, dtype=jnp.int32)[None, :]).astype(jnp.int32)
    page_rank = jnp.sum((jnp.cumsum(onehot, axis=0) - 1) * onehot, axis=1)
    target = page_group * group_pages + page_rank
    return (
        jnp.zeros((page_total,), jnp.int32).at[target].set(jnp.arange(page_total, dtype=jnp.int32))
    )


def attend_rows(query_rows, key_rows, value_rows, prefix_keys, prefix_values, length, head_total):
    row_count = query_rows.shape[0]
    features = query_rows.shape[1]
    head_size = features // head_total
    scale = head_size ** (-0.5)
    head_of_column = jnp.arange(features, dtype=jnp.int32) // head_size
    own_head = head_of_column[None, :] == jnp.arange(head_total, dtype=jnp.int32)[:, None]
    masked_queries = jnp.where(
        own_head[:, None, :], query_rows[None], jnp.zeros_like(query_rows)[None]
    ).reshape(head_total * row_count, features)
    prefix_scores = (
        jnp.dot(masked_queries, prefix_keys.T, preferred_element_type=jnp.float32) * scale
    ).reshape(head_total, row_count, -1)
    suffix_scores = (
        jnp.dot(masked_queries, key_rows.T, preferred_element_type=jnp.float32) * scale
    ).reshape(head_total, row_count, -1)
    query_pos = jnp.arange(row_count, dtype=jnp.int32)[:, None]
    key_pos = jnp.arange(row_count, dtype=jnp.int32)[None, :]
    allowed = (key_pos <= query_pos) & (key_pos < length)
    suffix_scores = jnp.where(allowed[None], suffix_scores, -jnp.inf)
    row_max = jnp.maximum(jnp.max(prefix_scores, axis=2), jnp.max(suffix_scores, axis=2))[..., None]
    prefix_exp = jnp.exp(prefix_scores - row_max)
    suffix_exp = jnp.exp(suffix_scores - row_max)
    denominators = jnp.sum(prefix_exp, axis=2, keepdims=True) + jnp.sum(
        suffix_exp, axis=2, keepdims=True
    )
    prefix_probs = (prefix_exp / denominators).astype(jnp.bfloat16)
    suffix_probs = (suffix_exp / denominators).astype(jnp.bfloat16)
    mixed = jnp.dot(
        prefix_probs.reshape(head_total * row_count, -1),
        prefix_values,
        preferred_element_type=jnp.float32,
    ) + jnp.dot(
        suffix_probs.reshape(head_total * row_count, -1),
        value_rows,
        preferred_element_type=jnp.float32,
    )
    mixed = mixed.reshape(head_total, row_count, features)
    picked = jnp.where(own_head[:, None, :], mixed, jnp.zeros_like(mixed))
    return jnp.sum(picked, axis=0).astype(jnp.bfloat16)


def slot_table(route_rows, replicas, per_device, experts):
    row_count, topk_count = route_rows.shape
    sub_rows = row_count // replicas
    flat_routes = route_rows.reshape(replicas, sub_rows * topk_count)
    onehot = (flat_routes[..., None] == jnp.arange(experts, dtype=jnp.int32)).astype(jnp.int32)
    slot_rank = jnp.sum((jnp.cumsum(onehot, axis=1) - 1) * onehot, axis=2).reshape(-1)
    expert_flat = route_rows.reshape(-1)
    block_of = jnp.arange(row_count * topk_count, dtype=jnp.int32) // (sub_rows * topk_count)
    target_device = expert_flat // per_device * replicas + block_of
    local_slot = expert_flat % per_device
    return (target_device, local_slot, slot_rank)


def on_device(
    hidden,
    queries,
    suffix_keys,
    suffix_values,
    lengths,
    key_cache,
    value_cache,
    page_group,
    out_weight,
    norm_gain,
    router_weight,
    routes,
    gate_weight,
    up_weight,
    down_weight,
    destinations,
):
    expert_count = lax.axis_size("ex")
    replica_count = lax.axis_size("rep")
    seq_count = expert_count * replica_count
    head_count = lax.axis_size("head")
    seq_index = lax.axis_index("ex") * replica_count + lax.axis_index("rep")
    head_index = lax.axis_index("head")
    row_count = hidden.shape[0]
    column_width = hidden.shape[1]
    features = queries.shape[1]
    local_heads = features // DH
    block_devices = seq_count // GROUPS
    page_local = key_cache.shape[0]
    page_rows = key_cache.shape[1]
    group_pages = page_local * block_devices
    capacity = row_count * TOPK // expert_count
    def head_ring(block):
        return [
            lax.ppermute(
                block,
                "head",
                [(source, (source + shift) % head_count) for source in range(head_count)],
            )
            for shift in range(1, head_count)
        ]

    rotated_weight = jnp.concatenate([out_weight] + head_ring(out_weight), axis=0)
    inverse = page_inverse(page_group, group_pages, GROUPS)
    inverse_destination = (
        jnp.zeros((seq_count,), jnp.int32)
        .at[destinations]
        .set(jnp.arange(seq_count, dtype=jnp.int32))
    )
    own_request = inverse_destination[seq_index]
    group_index = own_request // block_devices
    local_pages = jnp.concatenate([key_cache, value_cache], axis=2).reshape(
        page_local * page_rows, 2 * features
    )
    all_pages = lax.all_gather(local_pages, SEQ, axis=0, tiled=False).reshape(
        seq_count * page_local, page_rows, 2 * features
    )
    extra = jnp.zeros((row_count, 128), jnp.bfloat16)
    extra = extra.at[:, 0:TOPK].set(routes.astype(jnp.bfloat16))
    extra = extra.at[:, TOPK].set(lengths[0].astype(jnp.bfloat16))
    packed = jnp.concatenate([queries, suffix_keys, suffix_values, hidden, extra], axis=1)
    pieces = packed.reshape(seq_count, row_count // seq_count, packed.shape[1])
    spread = lax.all_to_all(pieces, SEQ, split_axis=0, concat_axis=0, tiled=True)
    spread = jnp.take(spread, inverse_destination, axis=0)
    moved = lax.all_to_all(spread, SEQ, split_axis=0, concat_axis=0, tiled=True).reshape(
        row_count, packed.shape[1]
    )
    queries = moved[:, 0:features]
    suffix_keys = moved[:, features : 2 * features]
    suffix_values = moved[:, 2 * features : 3 * features]
    hidden = moved[:, 3 * features : 3 * features + column_width]
    tail = 3 * features + column_width
    routes = moved[:, tail : tail + TOPK].astype(jnp.int32)
    length = moved[0, tail + TOPK].astype(jnp.int32)
    chosen = lax.dynamic_slice_in_dim(inverse, group_index * group_pages, group_pages, 0)
    held_pages = jnp.take(all_pages, chosen, axis=0)
    prefix_keys = held_pages[:, :, :features].reshape(group_pages * page_rows, features)
    prefix_values = held_pages[:, :, features:].reshape(group_pages * page_rows, features)
    attended = attend_rows(
        queries, suffix_keys, suffix_values, prefix_keys, prefix_values, length, local_heads
    )
    side = jnp.concatenate([hidden, router_weight.T], axis=0)
    rotated_side = jnp.stack([side] + head_ring(side), axis=0)
    source_head = (head_index - jnp.arange(head_count, dtype=jnp.int32)) % head_count
    side_blocks = jnp.take(rotated_side, source_head, axis=0)
    full_side = jnp.transpose(side_blocks, (1, 0, 2)).reshape(side.shape[0], head_count * features)
    full_hidden = full_side[:row_count]
    full_router = full_side[row_count:].T
    spread_attended = jnp.broadcast_to(attended[None], (head_count,) + attended.shape)
    by_source = lax.all_to_all(spread_attended, "head", split_axis=0, concat_axis=0, tiled=True)
    rotated_attended = jnp.transpose(jnp.take(by_source, source_head, axis=0), (1, 0, 2)).reshape(
        row_count, head_count * features
    )
    resid = full_hidden.astype(jnp.float32) + jnp.dot(
        rotated_attended, rotated_weight, preferred_element_type=jnp.float32
    )
    normed = (
        resid * lax.rsqrt(jnp.mean(resid * resid, axis=1, keepdims=True) + norm_eps) * norm_gain
    ).astype(jnp.bfloat16)
    logits = jnp.dot(normed, full_router, preferred_element_type=jnp.float32)
    chosen_logits = jnp.take_along_axis(logits, routes, axis=1)
    gate_first = jax.nn.sigmoid(chosen_logits[:, 0] - chosen_logits[:, 1])
    gate_second = jax.nn.sigmoid(chosen_logits[:, 1] - chosen_logits[:, 0])
    pair_count = row_count * TOPK
    expert_flat = routes.reshape(-1)
    onehot = (expert_flat[:, None] == jnp.arange(expert_count, dtype=jnp.int32)).astype(jnp.int32)
    slot_rank = jnp.sum((jnp.cumsum(onehot, axis=0) - 1) * onehot, axis=1)
    slot_flat = expert_flat * capacity + slot_rank
    slot_pair = (
        jnp.zeros((expert_count * capacity,), jnp.int32)
        .at[slot_flat]
        .set(jnp.arange(pair_count, dtype=jnp.int32), mode="drop")
    )
    send_rows = jnp.take(normed, slot_pair // TOPK, axis=0).reshape(
        expert_count, capacity, normed.shape[1]
    )
    slots = lax.all_to_all(send_rows, "ex", split_axis=0, concat_axis=0, tiled=True)
    slot_rows = slots.reshape(expert_count * capacity, slots.shape[2])
    gate_act = jnp.dot(slot_rows, gate_weight[0], preferred_element_type=jnp.float32)
    up_act = jnp.dot(slot_rows, up_weight[0], preferred_element_type=jnp.float32)
    expert_hidden = (jax.nn.gelu(gate_act, approximate=True) * up_act).astype(jnp.bfloat16)
    partial_out = lax.dot_general(
        expert_hidden,
        down_weight[0],
        (((1,), (1,)), ((), ())),
        preferred_element_type=jnp.float32,
    )
    split_part = jnp.transpose(
        partial_out.reshape(expert_count, capacity, head_count, column_width), (0, 2, 1, 3)
    ).astype(jnp.bfloat16)
    split_part = split_part.reshape(expert_count * head_count, capacity, column_width)
    arrived = lax.all_to_all(split_part, ("ex", "head"), split_axis=0, concat_axis=0, tiled=True)
    arrived = arrived.reshape(expert_count, head_count, capacity, column_width)
    returned = jnp.sum(arrived.astype(jnp.float32), axis=1).astype(jnp.bfloat16)
    picked = (
        returned[expert_flat, slot_rank].astype(jnp.float32).reshape(row_count, TOPK, column_width)
    )
    resid_columns = lax.dynamic_slice_in_dim(resid, head_index * column_width, column_width, 1)
    layer = resid_columns + gate_first[:, None] * picked[:, 0] + gate_second[:, None] * picked[:, 1]
    layer = layer.astype(jnp.bfloat16)
    live_rows = jnp.arange(row_count, dtype=jnp.int32) < length
    return jnp.where(live_rows[:, None], layer, jnp.zeros_like(layer))


SEQ = ("ex", "rep")


def solution(mesh):
    seq_count = mesh.shape["seq"]
    fine = Mesh(
        mesh.devices.reshape(EXPERTS, seq_count // EXPERTS, mesh.shape["head"]),
        ("ex", "rep", "head"),
    )
    return jax.shard_map(
        on_device,
        mesh=fine,
        in_specs=(
            P(SEQ, "head"),
            P(SEQ, "head"),
            P(SEQ, "head"),
            P(SEQ, "head"),
            P(SEQ),
            P(SEQ, None, "head"),
            P(SEQ, None, "head"),
            P(),
            P("head", None),
            P(),
            P("head", None),
            P(SEQ, None),
            P(SEQ, None, "head"),
            P(SEQ, None, "head"),
            P(SEQ, None, "head"),
            P(),
        ),
        out_specs=P(SEQ, "head"),
        check_vma=False,
    )
```

```python
import jax
import jax.numpy as jnp
from jax import lax
from jax.sharding import Mesh, PartitionSpec as P

DH = 64
EXPERTS = 16
TOPK = 2
GROUPS = 4


norm_eps = 1e-06


def page_inverse(page_group, group_pages, groups):
    page_total = page_group.shape[0]
    onehot = (page_group[:, None] == jnp.arange(groups, dtype=jnp.int32)[None, :]).astype(jnp.int32)
    page_rank = jnp.sum((jnp.cumsum(onehot, axis=0) - 1) * onehot, axis=1)
    target = page_group * group_pages + page_rank
    return (
        jnp.zeros((page_total,), jnp.int32).at[target].set(jnp.arange(page_total, dtype=jnp.int32))
    )


def attend_rows(query_rows, key_rows, value_rows, prefix_keys, prefix_values, length, head_total):
    row_count = query_rows.shape[0]
    features = query_rows.shape[1]
    head_size = features // head_total
    scale = head_size ** (-0.5)
    head_of_column = jnp.arange(features, dtype=jnp.int32) // head_size
    own_head = head_of_column[None, :] == jnp.arange(head_total, dtype=jnp.int32)[:, None]
    masked_queries = jnp.where(
        own_head[:, None, :], query_rows[None], jnp.zeros_like(query_rows)[None]
    ).reshape(head_total * row_count, features)
    prefix_scores = (
        jnp.dot(masked_queries, prefix_keys.T, preferred_element_type=jnp.float32) * scale
    ).reshape(head_total, row_count, -1)
    suffix_scores = (
        jnp.dot(masked_queries, key_rows.T, preferred_element_type=jnp.float32) * scale
    ).reshape(head_total, row_count, -1)
    query_pos = jnp.arange(row_count, dtype=jnp.int32)[:, None]
    key_pos = jnp.arange(row_count, dtype=jnp.int32)[None, :]
    allowed = (key_pos <= query_pos) & (key_pos < length)
    suffix_scores = jnp.where(allowed[None], suffix_scores, -jnp.inf)
    row_max = jnp.maximum(jnp.max(prefix_scores, axis=2), jnp.max(suffix_scores, axis=2))[..., None]
    prefix_exp = jnp.exp(prefix_scores - row_max)
    suffix_exp = jnp.exp(suffix_scores - row_max)
    denominators = jnp.sum(prefix_exp, axis=2, keepdims=True) + jnp.sum(
        suffix_exp, axis=2, keepdims=True
    )
    prefix_probs = (prefix_exp / denominators).astype(jnp.bfloat16)
    suffix_probs = (suffix_exp / denominators).astype(jnp.bfloat16)
    mixed = jnp.dot(
        prefix_probs.reshape(head_total * row_count, -1),
        prefix_values,
        preferred_element_type=jnp.float32,
    ) + jnp.dot(
        suffix_probs.reshape(head_total * row_count, -1),
        value_rows,
        preferred_element_type=jnp.float32,
    )
    mixed = mixed.reshape(head_total, row_count, features)
    picked = jnp.where(own_head[:, None, :], mixed, jnp.zeros_like(mixed))
    return jnp.sum(picked, axis=0).astype(jnp.bfloat16)


def slot_table(route_rows, replicas, per_device, experts):
    row_count, topk_count = route_rows.shape
    sub_rows = row_count // replicas
    flat_routes = route_rows.reshape(replicas, sub_rows * topk_count)
    onehot = (flat_routes[..., None] == jnp.arange(experts, dtype=jnp.int32)).astype(jnp.int32)
    slot_rank = jnp.sum((jnp.cumsum(onehot, axis=1) - 1) * onehot, axis=2).reshape(-1)
    expert_flat = route_rows.reshape(-1)
    block_of = jnp.arange(row_count * topk_count, dtype=jnp.int32) // (sub_rows * topk_count)
    target_device = expert_flat // per_device * replicas + block_of
    local_slot = expert_flat % per_device
    return (target_device, local_slot, slot_rank)


def on_device(
    hidden,
    queries,
    suffix_keys,
    suffix_values,
    lengths,
    key_cache,
    value_cache,
    page_group,
    out_weight,
    norm_gain,
    router_weight,
    routes,
    gate_weight,
    up_weight,
    down_weight,
    destinations,
):
    expert_count = lax.axis_size("ex")
    replica_count = lax.axis_size("rep")
    seq_count = expert_count * replica_count
    head_count = lax.axis_size("head")
    seq_index = lax.axis_index("ex") * replica_count + lax.axis_index("rep")
    head_index = lax.axis_index("head")
    row_count = hidden.shape[0]
    column_width = hidden.shape[1]
    features = queries.shape[1]
    local_heads = features // DH
    block_devices = seq_count // GROUPS
    page_local = key_cache.shape[0]
    page_rows = key_cache.shape[1]
    group_pages = page_local * block_devices
    capacity = row_count * TOPK // expert_count
    def head_ring(block):
        return [
            lax.ppermute(
                block,
                "head",
                [(source, (source + shift) % head_count) for source in range(head_count)],
            )
            for shift in range(1, head_count)
        ]

    rotated_weight = jnp.concatenate([out_weight] + head_ring(out_weight), axis=0)
    inverse = page_inverse(page_group, group_pages, GROUPS)
    inverse_destination = (
        jnp.zeros((seq_count,), jnp.int32)
        .at[destinations]
        .set(jnp.arange(seq_count, dtype=jnp.int32))
    )
    own_request = inverse_destination[seq_index]
    group_index = own_request // block_devices
    local_pages = jnp.concatenate([key_cache, value_cache], axis=2).reshape(
        page_local * page_rows, 2 * features
    )
    all_pages = lax.all_gather(local_pages, SEQ, axis=0, tiled=False).reshape(
        seq_count * page_local, page_rows, 2 * features
    )
    extra = jnp.zeros((row_count, 128), jnp.bfloat16)
    extra = extra.at[:, 0:TOPK].set(routes.astype(jnp.bfloat16))
    extra = extra.at[:, TOPK].set(lengths[0].astype(jnp.bfloat16))
    packed = jnp.concatenate([queries, suffix_keys, suffix_values, hidden, extra], axis=1)
    pieces = packed.reshape(seq_count, row_count // seq_count, packed.shape[1])
    spread = lax.all_to_all(pieces, SEQ, split_axis=0, concat_axis=0, tiled=True)
    spread = jnp.take(spread, inverse_destination, axis=0)
    moved = lax.all_to_all(spread, SEQ, split_axis=0, concat_axis=0, tiled=True).reshape(
        row_count, packed.shape[1]
    )
    queries = moved[:, 0:features]
    suffix_keys = moved[:, features : 2 * features]
    suffix_values = moved[:, 2 * features : 3 * features]
    hidden = moved[:, 3 * features : 3 * features + column_width]
    tail = 3 * features + column_width
    routes = moved[:, tail : tail + TOPK].astype(jnp.int32)
    length = moved[0, tail + TOPK].astype(jnp.int32)
    chosen = lax.dynamic_slice_in_dim(inverse, group_index * group_pages, group_pages, 0)
    held_pages = jnp.take(all_pages, chosen, axis=0)
    prefix_keys = held_pages[:, :, :features].reshape(group_pages * page_rows, features)
    prefix_values = held_pages[:, :, features:].reshape(group_pages * page_rows, features)
    attended = attend_rows(
        queries, suffix_keys, suffix_values, prefix_keys, prefix_values, length, local_heads
    )
    side = jnp.concatenate([hidden, router_weight.T], axis=0)
    rotated_side = jnp.stack([side] + head_ring(side), axis=0)
    source_head = (head_index - jnp.arange(head_count, dtype=jnp.int32)) % head_count
    side_blocks = jnp.take(rotated_side, source_head, axis=0)
    full_side = jnp.transpose(side_blocks, (1, 0, 2)).reshape(side.shape[0], head_count * features)
    full_hidden = full_side[:row_count]
    full_router = full_side[row_count:].T
    spread_attended = jnp.broadcast_to(attended[None], (head_count,) + attended.shape)
    by_source = lax.all_to_all(spread_attended, "head", split_axis=0, concat_axis=0, tiled=True)
    rotated_attended = jnp.transpose(jnp.take(by_source, source_head, axis=0), (1, 0, 2)).reshape(
        row_count, head_count * features
    )
    resid = full_hidden.astype(jnp.float32) + jnp.dot(
        rotated_attended, rotated_weight, preferred_element_type=jnp.float32
    )
    normed = (
        resid * lax.rsqrt(jnp.mean(resid * resid, axis=1, keepdims=True) + norm_eps) * norm_gain
    ).astype(jnp.bfloat16)
    logits = jnp.dot(normed, full_router, preferred_element_type=jnp.float32)
    chosen_logits = jnp.take_along_axis(logits, routes, axis=1)
    gate_first = jax.nn.sigmoid(chosen_logits[:, 0] - chosen_logits[:, 1])
    gate_second = jax.nn.sigmoid(chosen_logits[:, 1] - chosen_logits[:, 0])
    pair_count = row_count * TOPK
    expert_flat = routes.reshape(-1)
    onehot = (expert_flat[:, None] == jnp.arange(expert_count, dtype=jnp.int32)).astype(jnp.int32)
    slot_rank = jnp.sum((jnp.cumsum(onehot, axis=0) - 1) * onehot, axis=1)
    slot_flat = expert_flat * capacity + slot_rank
    slot_pair = (
        jnp.zeros((expert_count * capacity,), jnp.int32)
        .at[slot_flat]
        .set(jnp.arange(pair_count, dtype=jnp.int32), mode="drop")
    )
    send_pick = (
        (slot_pair // TOPK)[:, None] == jnp.arange(row_count, dtype=jnp.int32)[None, :]
    ).astype(jnp.bfloat16)
    send_rows = (
        jnp.dot(send_pick, normed, preferred_element_type=jnp.float32)
        .astype(jnp.bfloat16)
        .reshape(expert_count, capacity, normed.shape[1])
    )
    slots = lax.all_to_all(send_rows, "ex", split_axis=0, concat_axis=0, tiled=True)
    slot_rows = slots.reshape(expert_count * capacity, slots.shape[2])
    gate_act = jnp.dot(slot_rows, gate_weight[0], preferred_element_type=jnp.float32)
    up_act = jnp.dot(slot_rows, up_weight[0], preferred_element_type=jnp.float32)
    expert_hidden = (jax.nn.gelu(gate_act, approximate=True) * up_act).astype(jnp.bfloat16)
    partial_out = lax.dot_general(
        expert_hidden,
        down_weight[0],
        (((1,), (1,)), ((), ())),
        preferred_element_type=jnp.float32,
    )
    split_part = jnp.transpose(
        partial_out.reshape(expert_count, capacity, head_count, column_width), (0, 2, 1, 3)
    ).astype(jnp.bfloat16)
    split_part = split_part.reshape(expert_count * head_count, capacity, column_width)
    arrived = lax.all_to_all(split_part, ("ex", "head"), split_axis=0, concat_axis=0, tiled=True)
    arrived = arrived.reshape(expert_count, head_count, capacity, column_width)
    returned = jnp.sum(arrived.astype(jnp.float32), axis=1).astype(jnp.bfloat16)
    return_pick = (
        slot_flat[:, None] == jnp.arange(expert_count * capacity, dtype=jnp.int32)[None, :]
    ).astype(jnp.bfloat16)
    picked = jnp.dot(
        return_pick,
        returned.reshape(expert_count * capacity, column_width),
        preferred_element_type=jnp.float32,
    ).reshape(row_count, TOPK, column_width)
    resid_columns = lax.dynamic_slice_in_dim(resid, head_index * column_width, column_width, 1)
    layer = resid_columns + gate_first[:, None] * picked[:, 0] + gate_second[:, None] * picked[:, 1]
    layer = layer.astype(jnp.bfloat16)
    live_rows = jnp.arange(row_count, dtype=jnp.int32) < length
    return jnp.where(live_rows[:, None], layer, jnp.zeros_like(layer))


SEQ = ("ex", "rep")


def solution(mesh):
    seq_count = mesh.shape["seq"]
    fine = Mesh(
        mesh.devices.reshape(EXPERTS, seq_count // EXPERTS, mesh.shape["head"]),
        ("ex", "rep", "head"),
    )
    return jax.shard_map(
        on_device,
        mesh=fine,
        in_specs=(
            P(SEQ, "head"),
            P(SEQ, "head"),
            P(SEQ, "head"),
            P(SEQ, "head"),
            P(SEQ),
            P(SEQ, None, "head"),
            P(SEQ, None, "head"),
            P(),
            P("head", None),
            P(),
            P("head", None),
            P(SEQ, None),
            P(SEQ, None, "head"),
            P(SEQ, None, "head"),
            P(SEQ, None, "head"),
            P(),
        ),
        out_specs=P(SEQ, "head"),
        check_vma=False,
    )
```

```python
import jax
import jax.numpy as jnp
from jax import lax
from jax.sharding import Mesh, PartitionSpec as P

DH = 64
EXPERTS = 16
TOPK = 2
GROUPS = 4


norm_eps = 1e-06


def page_inverse(page_group, group_pages, groups):
    page_total = page_group.shape[0]
    onehot = (page_group[:, None] == jnp.arange(groups, dtype=jnp.int32)[None, :]).astype(jnp.int32)
    page_rank = jnp.sum((jnp.cumsum(onehot, axis=0) - 1) * onehot, axis=1)
    target = page_group * group_pages + page_rank
    return (
        jnp.zeros((page_total,), jnp.int32).at[target].set(jnp.arange(page_total, dtype=jnp.int32))
    )


def attend_rows(query_rows, key_rows, value_rows, prefix_keys, prefix_values, length, head_total):
    row_count = query_rows.shape[0]
    features = query_rows.shape[1]
    head_size = features // head_total
    scale = head_size ** (-0.5)
    head_of_column = jnp.arange(features, dtype=jnp.int32) // head_size
    own_head = head_of_column[None, :] == jnp.arange(head_total, dtype=jnp.int32)[:, None]
    masked_queries = jnp.where(
        own_head[:, None, :], query_rows[None], jnp.zeros_like(query_rows)[None]
    ).reshape(head_total * row_count, features)
    prefix_scores = (
        jnp.dot(masked_queries, prefix_keys.T, preferred_element_type=jnp.float32) * scale
    ).reshape(head_total, row_count, -1)
    suffix_scores = (
        jnp.dot(masked_queries, key_rows.T, preferred_element_type=jnp.float32) * scale
    ).reshape(head_total, row_count, -1)
    query_pos = jnp.arange(row_count, dtype=jnp.int32)[:, None]
    key_pos = jnp.arange(row_count, dtype=jnp.int32)[None, :]
    allowed = (key_pos <= query_pos) & (key_pos < length)
    suffix_scores = jnp.where(allowed[None], suffix_scores, -jnp.inf)
    row_max = jnp.maximum(jnp.max(prefix_scores, axis=2), jnp.max(suffix_scores, axis=2))[..., None]
    prefix_exp = jnp.exp(prefix_scores - row_max)
    suffix_exp = jnp.exp(suffix_scores - row_max)
    denominators = jnp.sum(prefix_exp, axis=2, keepdims=True) + jnp.sum(
        suffix_exp, axis=2, keepdims=True
    )
    prefix_probs = (prefix_exp / denominators).astype(jnp.bfloat16)
    suffix_probs = (suffix_exp / denominators).astype(jnp.bfloat16)
    mixed = jnp.dot(
        prefix_probs.reshape(head_total * row_count, -1),
        prefix_values,
        preferred_element_type=jnp.float32,
    ) + jnp.dot(
        suffix_probs.reshape(head_total * row_count, -1),
        value_rows,
        preferred_element_type=jnp.float32,
    )
    mixed = mixed.reshape(head_total, row_count, features)
    picked = jnp.where(own_head[:, None, :], mixed, jnp.zeros_like(mixed))
    return jnp.sum(picked, axis=0).astype(jnp.bfloat16)


def slot_table(route_rows, replicas, per_device, experts):
    row_count, topk_count = route_rows.shape
    sub_rows = row_count // replicas
    flat_routes = route_rows.reshape(replicas, sub_rows * topk_count)
    onehot = (flat_routes[..., None] == jnp.arange(experts, dtype=jnp.int32)).astype(jnp.int32)
    slot_rank = jnp.sum((jnp.cumsum(onehot, axis=1) - 1) * onehot, axis=2).reshape(-1)
    expert_flat = route_rows.reshape(-1)
    block_of = jnp.arange(row_count * topk_count, dtype=jnp.int32) // (sub_rows * topk_count)
    target_device = expert_flat // per_device * replicas + block_of
    local_slot = expert_flat % per_device
    return (target_device, local_slot, slot_rank)


def on_device(
    hidden,
    queries,
    suffix_keys,
    suffix_values,
    lengths,
    key_cache,
    value_cache,
    page_group,
    out_weight,
    norm_gain,
    router_weight,
    routes,
    gate_weight,
    up_weight,
    down_weight,
    destinations,
):
    expert_count = lax.axis_size("ex")
    replica_count = lax.axis_size("rep")
    seq_count = expert_count * replica_count
    head_count = lax.axis_size("head")
    seq_index = lax.axis_index("ex") * replica_count + lax.axis_index("rep")
    head_index = lax.axis_index("head")
    row_count = hidden.shape[0]
    column_width = hidden.shape[1]
    features = queries.shape[1]
    local_heads = features // DH
    block_devices = seq_count // GROUPS
    page_local = key_cache.shape[0]
    page_rows = key_cache.shape[1]
    group_pages = page_local * block_devices
    capacity = row_count * TOPK // expert_count
    def head_ring(block):
        return [
            lax.ppermute(
                block,
                "head",
                [(source, (source + shift) % head_count) for source in range(head_count)],
            )
            for shift in range(1, head_count)
        ]

    rotated_weight = jnp.concatenate([out_weight] + head_ring(out_weight), axis=0)
    inverse = page_inverse(page_group, group_pages, GROUPS)
    inverse_destination = (
        jnp.zeros((seq_count,), jnp.int32)
        .at[destinations]
        .set(jnp.arange(seq_count, dtype=jnp.int32))
    )
    own_request = inverse_destination[seq_index]
    group_index = own_request // block_devices
    local_pages = jnp.concatenate([key_cache, value_cache], axis=2).reshape(
        page_local * page_rows, 2 * features
    )
    all_pages = lax.all_gather(local_pages, SEQ, axis=0, tiled=False).reshape(
        seq_count * page_local, page_rows, 2 * features
    )
    extra = jnp.zeros((row_count, 128), jnp.bfloat16)
    extra = extra.at[:, 0:TOPK].set(routes.astype(jnp.bfloat16))
    extra = extra.at[:, TOPK].set(lengths[0].astype(jnp.bfloat16))
    packed = jnp.concatenate([queries, suffix_keys, suffix_values, hidden, extra], axis=1)
    pieces = packed.reshape(seq_count, row_count // seq_count, packed.shape[1])
    spread = lax.all_to_all(pieces, SEQ, split_axis=0, concat_axis=0, tiled=True)
    spread = jnp.take(spread, inverse_destination, axis=0)
    moved = lax.all_to_all(spread, SEQ, split_axis=0, concat_axis=0, tiled=True).reshape(
        row_count, packed.shape[1]
    )
    queries = moved[:, 0:features]
    suffix_keys = moved[:, features : 2 * features]
    suffix_values = moved[:, 2 * features : 3 * features]
    hidden = moved[:, 3 * features : 3 * features + column_width]
    tail = 3 * features + column_width
    routes = moved[:, tail : tail + TOPK].astype(jnp.int32)
    length = moved[0, tail + TOPK].astype(jnp.int32)
    chosen = lax.dynamic_slice_in_dim(inverse, group_index * group_pages, group_pages, 0)
    page_pick = (
        chosen[:, None] == jnp.arange(all_pages.shape[0], dtype=jnp.int32)[None, :]
    ).astype(jnp.bfloat16)
    held_pages = (
        jnp.dot(page_pick, all_pages.reshape(all_pages.shape[0], -1), preferred_element_type=jnp.float32)
        .astype(jnp.bfloat16)
        .reshape(group_pages, page_rows, all_pages.shape[2])
    )
    prefix_keys = held_pages[:, :, :features].reshape(group_pages * page_rows, features)
    prefix_values = held_pages[:, :, features:].reshape(group_pages * page_rows, features)
    attended = attend_rows(
        queries, suffix_keys, suffix_values, prefix_keys, prefix_values, length, local_heads
    )
    side = jnp.concatenate([hidden, router_weight.T], axis=0)
    rotated_side = jnp.stack([side] + head_ring(side), axis=0)
    source_head = (head_index - jnp.arange(head_count, dtype=jnp.int32)) % head_count
    side_blocks = jnp.take(rotated_side, source_head, axis=0)
    full_side = jnp.transpose(side_blocks, (1, 0, 2)).reshape(side.shape[0], head_count * features)
    full_hidden = full_side[:row_count]
    full_router = full_side[row_count:].T
    spread_attended = jnp.broadcast_to(attended[None], (head_count,) + attended.shape)
    by_source = lax.all_to_all(spread_attended, "head", split_axis=0, concat_axis=0, tiled=True)
    rotated_attended = jnp.transpose(jnp.take(by_source, source_head, axis=0), (1, 0, 2)).reshape(
        row_count, head_count * features
    )
    resid = full_hidden.astype(jnp.float32) + jnp.dot(
        rotated_attended, rotated_weight, preferred_element_type=jnp.float32
    )
    normed = (
        resid * lax.rsqrt(jnp.mean(resid * resid, axis=1, keepdims=True) + norm_eps) * norm_gain
    ).astype(jnp.bfloat16)
    logits = jnp.dot(normed, full_router, preferred_element_type=jnp.float32)
    chosen_logits = jnp.take_along_axis(logits, routes, axis=1)
    gate_first = jax.nn.sigmoid(chosen_logits[:, 0] - chosen_logits[:, 1])
    gate_second = jax.nn.sigmoid(chosen_logits[:, 1] - chosen_logits[:, 0])
    pair_count = row_count * TOPK
    expert_flat = routes.reshape(-1)
    onehot = (expert_flat[:, None] == jnp.arange(expert_count, dtype=jnp.int32)).astype(jnp.int32)
    slot_rank = jnp.sum((jnp.cumsum(onehot, axis=0) - 1) * onehot, axis=1)
    slot_flat = expert_flat * capacity + slot_rank
    slot_pair = (
        jnp.zeros((expert_count * capacity,), jnp.int32)
        .at[slot_flat]
        .set(jnp.arange(pair_count, dtype=jnp.int32), mode="drop")
    )
    send_pick = (
        (slot_pair // TOPK)[:, None] == jnp.arange(row_count, dtype=jnp.int32)[None, :]
    ).astype(jnp.bfloat16)
    send_rows = (
        jnp.dot(send_pick, normed, preferred_element_type=jnp.float32)
        .astype(jnp.bfloat16)
        .reshape(expert_count, capacity, normed.shape[1])
    )
    slots = lax.all_to_all(send_rows, "ex", split_axis=0, concat_axis=0, tiled=True)
    slot_rows = slots.reshape(expert_count * capacity, slots.shape[2])
    gate_act = jnp.dot(slot_rows, gate_weight[0], preferred_element_type=jnp.float32)
    up_act = jnp.dot(slot_rows, up_weight[0], preferred_element_type=jnp.float32)
    expert_hidden = (jax.nn.gelu(gate_act, approximate=True) * up_act).astype(jnp.bfloat16)
    partial_out = lax.dot_general(
        expert_hidden,
        down_weight[0],
        (((1,), (1,)), ((), ())),
        preferred_element_type=jnp.float32,
    )
    split_part = jnp.transpose(
        partial_out.reshape(expert_count, capacity, head_count, column_width), (0, 2, 1, 3)
    ).astype(jnp.bfloat16)
    split_part = split_part.reshape(expert_count * head_count, capacity, column_width)
    arrived = lax.all_to_all(split_part, ("ex", "head"), split_axis=0, concat_axis=0, tiled=True)
    arrived = arrived.reshape(expert_count, head_count, capacity, column_width)
    returned = jnp.sum(arrived.astype(jnp.float32), axis=1).astype(jnp.bfloat16)
    return_pick = (
        slot_flat[:, None] == jnp.arange(expert_count * capacity, dtype=jnp.int32)[None, :]
    ).astype(jnp.bfloat16)
    picked = jnp.dot(
        return_pick,
        returned.reshape(expert_count * capacity, column_width),
        preferred_element_type=jnp.float32,
    ).reshape(row_count, TOPK, column_width)
    resid_columns = lax.dynamic_slice_in_dim(resid, head_index * column_width, column_width, 1)
    layer = resid_columns + gate_first[:, None] * picked[:, 0] + gate_second[:, None] * picked[:, 1]
    layer = layer.astype(jnp.bfloat16)
    live_rows = jnp.arange(row_count, dtype=jnp.int32) < length
    return jnp.where(live_rows[:, None], layer, jnp.zeros_like(layer))


SEQ = ("ex", "rep")


def solution(mesh):
    seq_count = mesh.shape["seq"]
    fine = Mesh(
        mesh.devices.reshape(EXPERTS, seq_count // EXPERTS, mesh.shape["head"]),
        ("ex", "rep", "head"),
    )
    return jax.shard_map(
        on_device,
        mesh=fine,
        in_specs=(
            P(SEQ, "head"),
            P(SEQ, "head"),
            P(SEQ, "head"),
            P(SEQ, "head"),
            P(SEQ),
            P(SEQ, None, "head"),
            P(SEQ, None, "head"),
            P(),
            P("head", None),
            P(),
            P("head", None),
            P(SEQ, None),
            P(SEQ, None, "head"),
            P(SEQ, None, "head"),
            P(SEQ, None, "head"),
            P(),
        ),
        out_specs=P(SEQ, "head"),
        check_vma=False,
    )
```
